128 devices in a mesh: tm: 32 (over x, z_hi, y), qband: 4 (over z_lo, core).
Axes of the slice: x: 4, y: 4, z: 4 (z_hi: 2, z_lo: 2; z = z_hi * 2 + z_lo), core: 2. Of those that a mesh axis runs over, the one named last changes fastest.
Arguments:
- frames: bfloat16 [128, 1024, 1024], P(('tm', 'qband')), may hold values from -8 to 8
- lag_list: int32 [16], replicated, may hold values from 1 to 64, as said below
- band_index: int32 [1024, 1], P(('tm', 'qband')), may hold values from 0 to 63
- decay_rates: float32 [64, 1024], P('tm', 'qband'), may hold values from 0.002 to 1
Outputs:
- structure: float32 [16, 1024, 1024], P(None, ('tm', 'qband'))
- weights: float32 [64, 1024], P('tm', 'qband')
The draws below stay inside these ranges and needn't reach their ends.
Inputs may be any that keep to these rules, and one draw needn't show every extreme that they name: `lag_list`: 16 different lags, the largest exactly 64. `band_index`: every band has at least one row.
All inputs are finite; a program needn't handle non-finite values.
Results may differ from the reference program's by a relative error of at most 0.0018.
Values may be sent and summed in bfloat16 or wider, within the bound.
No kernel may reach another device: no remote copies, remote signals or barrier semaphores. Data moves between devices by JAX's collectives and lax.ppermute only.
A program may use at most 128 MiB of HBM per device.

```python
import math
import jax
import jax.numpy as jnp
from jax import lax

PIX = 1024
NLAG = 16
BINS = 1024
ITERS = 64
FRAMES = 128
NB = 64


def draw_frames(key, part):
    keys = jax.random.split(key, 4)
    amplitude = jax.random.normal(keys[0], (PIX, PIX), jnp.float32)
    frequency = jnp.exp(jax.random.uniform(keys[1], (PIX, PIX), jnp.float32, jnp.log(0.5 / FRAMES), jnp.log(2.0)))
    offset = jax.random.uniform(keys[2], (PIX, PIX), jnp.float32, -math.pi, math.pi)
    noise = jax.random.normal(keys[3], (FRAMES, PIX, PIX), jnp.float32)
    moments = jnp.arange(FRAMES, dtype=jnp.float32)[:, None, None]
    values = 1.2 * amplitude[None] * jnp.cos(frequency[None] * moments + offset[None]) + 0.5 * noise
    return jnp.clip(values, -8.0, 8.0).astype(jnp.bfloat16)


def draw_lag_list(key, part):
    shuffled = jax.random.permutation(key, FRAMES // 2 - 1) + 1
    largest = jnp.full((1,), FRAMES // 2, dtype=jnp.int32)
    return jnp.concatenate([shuffled[:NLAG - 1].astype(jnp.int32), largest])


def block_scale(rng, extent, pieces, least, top_value):
    def one(axis_at, parts):
        steps = jax.random.uniform(jax.random.fold_in(jax.random.fold_in(rng, 6), axis_at), (parts,), jnp.float32, least / len(pieces), top_value / len(pieces))
        return jnp.repeat(jnp.exp(steps), extent[axis_at] // parts).reshape((-1,) + (1,) * (len(extent) - axis_at - 1))

    factor_of = one(*pieces[0])
    for cut in pieces[1:]:
        factor_of = factor_of * one(*cut)
    return factor_of


def picks_of(own_key, rows, number_of, top, lift):
    sequence = jax.random.permutation(jax.random.fold_in(own_key, 1), number_of)
    favour = sequence
    for power in range(3):
        favour = favour * favour // number_of
    favour = favour * lift // number_of
    tickets = jax.random.randint(jax.random.fold_in(own_key, 2), (rows, number_of), 0, 4096) + favour
    holders = jax.random.permutation(jax.random.fold_in(own_key, 3), rows)[jnp.arange(number_of) % rows]
    tickets = jnp.where(jnp.arange(rows)[:, None] == holders[None, :], 1 << 14, tickets)
    priority = tickets * number_of + jnp.arange(number_of)
    return lax.top_k(priority.astype(jnp.int32), top)[1].astype(jnp.int32)


def setup_inputs(seed: int = 0) -> dict:
    arg_keys = jax.random.split(jax.random.key(seed), 5)
    frames = draw_frames(jax.random.fold_in(arg_keys[4], 71), 0)
    lag_list = draw_lag_list(jax.random.fold_in(arg_keys[4], 71), 0)
    band_index = picks_of(arg_keys[2], PIX, NB, 1, 0)
    decay_rates = jnp.clip(jnp.exp(math.log(1.0) - 6.214608 * jax.random.uniform(arg_keys[3], (NB, BINS), jnp.float32) ** block_scale(arg_keys[3], (NB, BINS), ((0, 32), (1, 4)), -0.2, 0.2)), 0.002, 1.0)
    return {"frames": frames, "lag_list": lag_list, "band_index": band_index, "decay_rates": decay_rates}


def dft_table(length):
    positions = jnp.arange(length, dtype=jnp.int32)
    phase_index = positions[:, None] * positions[None, :] % length
    folded = jnp.minimum(phase_index, length - phase_index)
    sign_factor = jnp.where(phase_index * 2 > length, -1.0, 1.0).astype(jnp.float32)
    angles = folded.astype(jnp.float32) * (2.0 * math.pi / length)
    factor = 1.0 / math.sqrt(length)
    return jnp.concatenate([jnp.cos(angles) * factor, -sign_factor * jnp.sin(angles) * factor], axis=1).astype(jnp.bfloat16)

def transform_frame(image, table):
    pixels = image.shape[0]
    rows_done = jnp.dot(image, table, preferred_element_type=jnp.float32).astype(jnp.bfloat16)
    real_rows = rows_done[:, :pixels].T
    imag_rows = rows_done[:, pixels:].T
    first = jnp.dot(real_rows, table, preferred_element_type=jnp.float32)
    second = jnp.dot(imag_rows, table, preferred_element_type=jnp.float32)
    spec_real = first[:, :pixels] - second[:, pixels:]
    spec_imag = first[:, pixels:] + second[:, :pixels]
    return jnp.stack([spec_real, spec_imag]).astype(jnp.bfloat16)

def structure_block(spectrum_block, lag_list):
    frames_all = spectrum_block.shape[2]
    padded = jnp.concatenate([spectrum_block, jnp.zeros_like(spectrum_block)], axis=2)
    time_index = jnp.arange(frames_all, dtype=jnp.int32)

    def one_lag(lag_value):
        shifted = lax.dynamic_slice_in_dim(padded, lag_value, frames_all, 2)
        difference = shifted.astype(jnp.float32) - spectrum_block.astype(jnp.float32)
        squared = difference[0] * difference[0] + difference[1] * difference[1]
        in_range = (time_index < frames_all - lag_value).astype(jnp.float32)
        summed = lax.optimization_barrier(jnp.sum(squared * in_range[None, :, None], axis=1))
        return summed / (frames_all - lag_value).astype(jnp.float32)
    return lax.map(one_lag, lag_list)

def reference(frames, lag_list, band_index, decay_rates):
    table = dft_table(PIX)
    spectra = lax.map(lambda image: transform_frame(image, table), frames)
    spectrum = jnp.transpose(spectra, (1, 2, 0, 3))
    block_rows = 64 if PIX % 64 == 0 else PIX
    block_count = PIX // block_rows
    blocked = jnp.transpose(spectrum.reshape(2, block_count, block_rows, FRAMES, PIX), (1, 0, 2, 3, 4))
    measured = lax.map(lambda block_data: structure_block(block_data, lag_list), blocked)
    structure = jnp.transpose(measured, (1, 0, 2, 3)).reshape(NLAG, PIX, PIX)
    row_sums = lax.optimization_barrier(jnp.sum(structure, axis=2))
    band_ids = jnp.arange(NB, dtype=jnp.int32)
    one_hot = (band_index[:, 0][None, :] == band_ids[:, None]).astype(jnp.float32)
    totals = jnp.dot(one_hot, row_sums.T, precision=lax.Precision.HIGHEST)
    counts = lax.optimization_barrier(jnp.sum(one_hot, axis=1))
    band_mean = totals / (counts[:, None] * PIX)
    lag_values = lag_list.astype(jnp.float32)
    kernel = (1.0 - jnp.exp(-decay_rates[:, None, :] * lag_values[None, :, None])) / BINS
    step_size = 1.0 / lax.optimization_barrier(jnp.sum(kernel * kernel, axis=(1, 2)))

    def iterate(counter, weights):
        predicted = jnp.einsum('blk,bk->bl', kernel, weights, precision=lax.Precision.HIGHEST)
        residual = predicted - band_mean
        gradient = jnp.einsum('blk,bl->bk', kernel, residual, precision=lax.Precision.HIGHEST)
        return jnp.maximum(weights - step_size[:, None] * gradient, 0.0)
    weights = lax.fori_loop(0, ITERS, iterate, jnp.zeros((NB, BINS), jnp.float32))
    return (structure, weights)
```

```python
import math

import jax
import jax.numpy as jnp
from jax import lax
from jax.sharding import PartitionSpec as P
from jax.experimental import pallas as pl
from jax.experimental.pallas import tpu as pltpu

BINS = 1024
ITERS = 64


def dft_table(length):
    positions = jnp.arange(length, dtype=jnp.int32)
    phase_index = positions[:, None] * positions[None, :] % length
    folded = jnp.minimum(phase_index, length - phase_index)
    sign_factor = jnp.where(phase_index * 2 > length, -1.0, 1.0).astype(jnp.float32)
    angles = folded.astype(jnp.float32) * (2.0 * math.pi / length)
    factor = 1.0 / math.sqrt(length)
    return jnp.concatenate(
        [jnp.cos(angles) * factor, -sign_factor * jnp.sin(angles) * factor], axis=1
    ).astype(jnp.bfloat16)


def structure_block(spectrum_block, lag_list):
    frames_all = spectrum_block.shape[2]
    padded = jnp.concatenate([spectrum_block, jnp.zeros_like(spectrum_block)], axis=2)
    time_index = jnp.arange(frames_all, dtype=jnp.int32)

    def one_lag(lag_value):
        shifted = lax.dynamic_slice_in_dim(padded, lag_value, frames_all, 2)
        difference = shifted.astype(jnp.float32) - spectrum_block.astype(jnp.float32)
        squared = difference[0] * difference[0] + difference[1] * difference[1]
        in_range = (time_index < frames_all - lag_value).astype(jnp.float32)
        summed = jnp.sum(squared * in_range[None, :, None], axis=1)
        return summed / (frames_all - lag_value).astype(jnp.float32)

    return lax.map(one_lag, lag_list)


def kernel_panel(decay_rates, lag_list):
    lag_values = lag_list.astype(jnp.float32)
    return (1.0 - jnp.exp(-decay_rates[:, None, :] * lag_values[None, :, None])) / BINS


def descend(kernel, target, step_size, weights, combine):
    partial_value = jnp.einsum("blk,bk->bl", kernel, weights, precision=lax.Precision.HIGHEST)
    residual = combine(partial_value) - target
    gradient = jnp.einsum("blk,bl->bk", kernel, residual, precision=lax.Precision.HIGHEST)
    return jnp.maximum(weights - step_size[:, None] * gradient, 0.0)


def on_device(frames, lag_list, band_index, decay_rates):
    frames_dev, pixels = (frames.shape[0], frames.shape[1])
    table = dft_table(pixels)
    row_transform = jnp.einsum("xk,tyx->kty", table, frames, preferred_element_type=jnp.float32)
    row_transform = row_transform.reshape(2, pixels, frames_dev, pixels).astype(jnp.bfloat16)
    products = jnp.einsum("ckty,yj->cktj", row_transform, table, preferred_element_type=jnp.float32)
    spec_real = products[0, :, :, :pixels] - products[1, :, :, pixels:]
    spec_imag = products[0, :, :, pixels:] + products[1, :, :, :pixels]
    spectrum = jnp.stack([spec_real, spec_imag]).astype(jnp.bfloat16)
    structure = structure_block(
        lax.all_to_all(spectrum, ("tm", "qband"), split_axis=1, concat_axis=2, tiled=True), lag_list
    )
    bands_dev = decay_rates.shape[0]
    bands_total = bands_dev * lax.axis_size("tm")
    row_sums = jnp.sum(structure, axis=2)
    band_ids = jnp.arange(bands_total, dtype=jnp.int32)
    one_hot = (band_index[:, 0][None, :] == band_ids[:, None]).astype(jnp.float32)
    partial_totals = jnp.dot(one_hot, row_sums.T, precision=lax.Precision.HIGHEST)
    partial_counts = jnp.sum(one_hot, axis=1)
    totals, counts = lax.psum((partial_totals, partial_counts), ("tm", "qband"))
    band_mean = totals / (counts[:, None] * pixels)
    target = lax.dynamic_slice_in_dim(band_mean, lax.axis_index("tm") * bands_dev, bands_dev, 0)
    columns = decay_rates.shape[1]
    all_rates = lax.all_gather(decay_rates, "qband", axis=1, tiled=True)
    kernel = kernel_panel(all_rates, lag_list)
    step_size = 1.0 / jnp.sum(kernel * kernel, axis=(1, 2))
    weights = fit_bands(kernel, target, step_size)
    weights = lax.dynamic_slice_in_dim(weights, lax.axis_index("qband") * columns, columns, 1)
    return (structure, weights)


def fit_kernel(k_ref, tgt_ref, step_ref, w_ref):
    for b in range(k_ref.shape[0]):
        panel = k_ref[b]
        tgt = tgt_ref[b][:, 0:1]
        step = step_ref[b]

        def body(i, w):
            predicted = jnp.sum(panel * w, axis=1, keepdims=True)
            residual = predicted - tgt
            gradient = jnp.sum(panel * residual, axis=0, keepdims=True)
            return jnp.maximum(w - step * gradient, 0.0)

        w_ref[b] = lax.fori_loop(0, ITERS, body, jnp.zeros(step.shape, jnp.float32))


def fit_bands(kernel, target, step_size):
    bands, lags, bins = kernel.shape
    tgt = jnp.broadcast_to(target[:, :, None], (bands, lags, 128))
    step = jnp.broadcast_to(step_size[:, None, None], (bands, 1, bins))
    out = pl.pallas_call(
        fit_kernel,
        out_shape=jax.ShapeDtypeStruct((bands, 1, bins), jnp.float32),
    )(kernel, tgt, step)
    return out[:, 0, :]


def solution(mesh):
    placed = (P(("tm", "qband"), None, None), P(), P(("tm", "qband"), None), P("tm", "qband"))
    return jax.shard_map(
        on_device,
        mesh=mesh,
        in_specs=placed,
        out_specs=(P(None, ("tm", "qband"), None), P("tm", "qband")),
        check_vma=False,
    )
```

```python
import math

import jax
import jax.numpy as jnp
from jax import lax
from jax.sharding import PartitionSpec as P
from jax.experimental import pallas as pl
from jax.experimental.pallas import tpu as pltpu

BINS = 1024
ITERS = 64


def dft_table(length):
    positions = jnp.arange(length, dtype=jnp.int32)
    phase_index = positions[:, None] * positions[None, :] % length
    folded = jnp.minimum(phase_index, length - phase_index)
    sign_factor = jnp.where(phase_index * 2 > length, -1.0, 1.0).astype(jnp.float32)
    angles = folded.astype(jnp.float32) * (2.0 * math.pi / length)
    factor = 1.0 / math.sqrt(length)
    return jnp.concatenate(
        [jnp.cos(angles) * factor, -sign_factor * jnp.sin(angles) * factor], axis=1
    ).astype(jnp.bfloat16)


def structure_kernel(lags_ref, x_ref, out_ref, x32_ref):
    frames_all = x_ref.shape[0]

    def convert(t, carry):
        x32_ref[t] = x_ref[t].astype(jnp.float32)
        return carry

    lax.fori_loop(0, frames_all, convert, 0)

    def one_lag(l, carry):
        lag = lags_ref[l]
        count = frames_all - lag

        def step(t, acc):
            d = x32_ref[t + lag] - x32_ref[t]
            return acc + d * d

        out_ref[l] = lax.fori_loop(0, count, step, jnp.zeros(x32_ref.shape[1:], jnp.float32))
        return carry

    lax.fori_loop(0, lags_ref.shape[0], one_lag, 0)


def structure_block(spectrum_block, lag_list):
    frames_all, rows, pixels = spectrum_block.shape
    nlag = lag_list.shape[0]
    summed = pl.pallas_call(
        structure_kernel,
        out_shape=jax.ShapeDtypeStruct((nlag, rows, pixels), jnp.float32),
        in_specs=[
            pl.BlockSpec(memory_space=pltpu.SMEM),
            pl.BlockSpec(memory_space=pltpu.VMEM),
        ],
        out_specs=pl.BlockSpec(memory_space=pltpu.VMEM),
        scratch_shapes=[
            pltpu.VMEM((frames_all, rows, pixels), jnp.float32),
        ],
        compiler_params=pltpu.CompilerParams(vmem_limit_bytes=40 * 1024 * 1024),
    )(lag_list, spectrum_block)
    summed = jnp.sum(summed.reshape(nlag, rows // 2, 2, pixels), axis=2)
    return summed / (frames_all - lag_list).astype(jnp.float32)[:, None, None]


def kernel_panel(decay_rates, lag_list):
    lag_values = lag_list.astype(jnp.float32)
    return (1.0 - jnp.exp(-decay_rates[:, None, :] * lag_values[None, :, None])) / BINS


def fit_kernel(k_ref, tgt_ref, step_ref, w_ref):
    for b in range(k_ref.shape[0]):
        panel = k_ref[b]
        tgt = tgt_ref[b][:, 0:1]
        step = step_ref[b]

        def body(i, w):
            predicted = jnp.sum(panel * w, axis=1, keepdims=True)
            residual = predicted - tgt
            gradient = jnp.sum(panel * residual, axis=0, keepdims=True)
            return jnp.maximum(w - step * gradient, 0.0)

        w_ref[b] = lax.fori_loop(0, ITERS, body, jnp.zeros(step.shape, jnp.float32))


def fit_bands(kernel, target, step_size):
    bands, lags, bins = kernel.shape
    tgt = jnp.broadcast_to(target[:, :, None], (bands, lags, 128))
    step = jnp.broadcast_to(step_size[:, None, None], (bands, 1, bins))
    out = pl.pallas_call(
        fit_kernel,
        out_shape=jax.ShapeDtypeStruct((bands, 1, bins), jnp.float32),
    )(kernel, tgt, step)
    return out[:, 0, :]


def on_device(frames, lag_list, band_index, decay_rates):
    pixels = frames.shape[1]
    devices = lax.axis_size(("tm", "qband"))
    table = dft_table(pixels)
    index_all = lax.all_gather(band_index[:, 0].astype(jnp.float32), ("tm", "qband"), axis=0, tiled=True)
    row_transform = jnp.dot(frames[0], table, preferred_element_type=jnp.float32).astype(jnp.bfloat16)
    row_transform = row_transform.reshape(pixels, 2, pixels)
    cos_part = table[:, :pixels]
    sin_part = table[:, pixels:]
    mixing = jnp.stack([table, jnp.concatenate([-sin_part, cos_part], axis=1)])
    spectrum = jnp.einsum("ypk,pyj->kj", row_transform, mixing, preferred_element_type=jnp.float32)
    spectrum = spectrum.astype(jnp.bfloat16).reshape(devices, (pixels // devices) * 2, pixels)
    gathered = lax.all_to_all(spectrum, ("tm", "qband"), 0, 0, tiled=True)
    structure = structure_block(gathered, lag_list)

    bands_dev = decay_rates.shape[0]
    row_sums = jnp.sum(structure, axis=2)
    sums_all = lax.all_gather(row_sums, ("tm", "qband"), axis=1, tiled=True)
    own_bands = (lax.axis_index("tm") * bands_dev + jnp.arange(bands_dev, dtype=jnp.int32)).astype(jnp.float32)
    one_hot = (index_all[None, :] == own_bands[:, None]).astype(jnp.float32)
    totals = jnp.dot(one_hot, sums_all.T, precision=lax.Precision.HIGHEST)
    counts = jnp.sum(one_hot, axis=1)
    target = totals / (counts[:, None] * pixels)

    columns = decay_rates.shape[1]
    all_rates = lax.all_gather(decay_rates, "qband", axis=1, tiled=True)
    kernel = kernel_panel(all_rates, lag_list)
    step_size = 1.0 / jnp.sum(kernel * kernel, axis=(1, 2))
    weights = fit_bands(kernel, target, step_size)
    weights = lax.dynamic_slice_in_dim(weights, lax.axis_index("qband") * columns, columns, 1)
    return (structure, weights)


def solution(mesh):
    placed = (P(("tm", "qband"), None, None), P(), P(("tm", "qband"), None), P("tm", "qband"))
    return jax.shard_map(
        on_device,
        mesh=mesh,
        in_specs=placed,
        out_specs=(P(None, ("tm", "qband"), None), P("tm", "qband")),
        check_vma=False,
    )
```

```python
import math

import jax
import jax.numpy as jnp
from jax import lax
from jax.sharding import PartitionSpec as P
from jax.experimental import pallas as pl
from jax.experimental.pallas import tpu as pltpu

BINS = 1024
ITERS = 64


def dft_table(length):
    positions = jnp.arange(length, dtype=jnp.int32)
    phase_index = positions[:, None] * positions[None, :] % length
    folded = jnp.minimum(phase_index, length - phase_index)
    sign_factor = jnp.where(phase_index * 2 > length, -1.0, 1.0).astype(jnp.float32)
    angles = folded.astype(jnp.float32) * (2.0 * math.pi / length)
    factor = 1.0 / math.sqrt(length)
    return jnp.concatenate(
        [jnp.cos(angles) * factor, -sign_factor * jnp.sin(angles) * factor], axis=1
    ).astype(jnp.bfloat16)


def structure_kernel(lags_ref, x_ref, out_ref, x32_ref):
    frames_all = x_ref.shape[0]

    def convert(t, carry):
        x32_ref[t] = x_ref[t].astype(jnp.float32)
        return carry

    lax.fori_loop(0, frames_all, convert, 0)

    def one_lag(l, carry):
        lag = lags_ref[l]
        count = frames_all - lag

        def step(t, acc):
            d = x32_ref[t + lag] - x32_ref[t]
            return acc + d * d

        out_ref[l] = lax.fori_loop(0, count, step, jnp.zeros(x32_ref.shape[1:], jnp.float32))
        return carry

    lax.fori_loop(0, lags_ref.shape[0], one_lag, 0)


def structure_block(spectrum_block, lag_list):
    frames_all, rows, pixels = spectrum_block.shape
    nlag = lag_list.shape[0]
    summed = pl.pallas_call(
        structure_kernel,
        out_shape=jax.ShapeDtypeStruct((nlag, rows, pixels), jnp.float32),
        in_specs=[
            pl.BlockSpec(memory_space=pltpu.SMEM),
            pl.BlockSpec(memory_space=pltpu.VMEM),
        ],
        out_specs=pl.BlockSpec(memory_space=pltpu.VMEM),
        scratch_shapes=[
            pltpu.VMEM((frames_all, rows, pixels), jnp.float32),
        ],
        compiler_params=pltpu.CompilerParams(vmem_limit_bytes=40 * 1024 * 1024),
    )(lag_list, spectrum_block)
    summed = jnp.sum(summed.reshape(nlag, rows // 2, 2, pixels), axis=2)
    return summed / (frames_all - lag_list).astype(jnp.float32)[:, None, None]


def kernel_panel(decay_rates, lag_list):
    lag_values = lag_list.astype(jnp.float32)
    return (1.0 - jnp.exp(-decay_rates[:, None, :] * lag_values[None, :, None])) / BINS


def fit_kernel(k_ref, tgt_ref, step_ref, w_ref):
    for b in range(k_ref.shape[0]):
        panel = k_ref[b]
        tgt = tgt_ref[b][:, 0:1]
        step = step_ref[b]

        def body(i, w):
            predicted = jnp.sum(panel * w, axis=1, keepdims=True)
            residual = predicted - tgt
            gradient = jnp.sum(panel * residual, axis=0, keepdims=True)
            return jnp.maximum(w - step * gradient, 0.0)

        w_ref[b] = lax.fori_loop(0, ITERS, body, jnp.zeros(step.shape, jnp.float32))


def fit_bands(kernel, target, step_size):
    bands, lags, bins = kernel.shape
    tgt = jnp.broadcast_to(target[:, :, None], (bands, lags, 128))
    step = jnp.broadcast_to(step_size[:, None, None], (bands, 1, bins))
    out = pl.pallas_call(
        fit_kernel,
        out_shape=jax.ShapeDtypeStruct((bands, 1, bins), jnp.float32),
    )(kernel, tgt, step)
    return out[:, 0, :]


def on_device(frames, lag_list, band_index, decay_rates):
    pixels = frames.shape[1]
    devices = lax.axis_size(("tm", "qband"))
    table = dft_table(pixels)
    row_transform = jnp.dot(frames[0], table, preferred_element_type=jnp.float32).astype(jnp.bfloat16)
    row_transform = row_transform.reshape(pixels, 2, pixels)
    cos_part = table[:, :pixels]
    sin_part = table[:, pixels:]
    mixing = jnp.stack([table, jnp.concatenate([-sin_part, cos_part], axis=1)])
    spectrum = jnp.einsum("ypk,pyj->kj", row_transform, mixing, preferred_element_type=jnp.float32)
    spectrum = spectrum.astype(jnp.bfloat16).reshape(devices, (pixels // devices) * 2, pixels)
    gathered = lax.all_to_all(spectrum, ("tm", "qband"), 0, 0, tiled=True)
    structure = structure_block(gathered, lag_list)

    bands_dev = decay_rates.shape[0]
    bands_total = bands_dev * lax.axis_size("tm")
    row_sums = jnp.sum(structure, axis=2)
    band_ids = jnp.arange(bands_total, dtype=jnp.int32)
    one_hot = (band_index[:, 0][None, :] == band_ids[:, None]).astype(jnp.float32)
    partial_totals = jnp.dot(one_hot, row_sums.T, precision=lax.Precision.HIGHEST)
    partial_counts = jnp.sum(one_hot, axis=1, keepdims=True)
    partial = jnp.concatenate([partial_totals, partial_counts], axis=1)
    per_dest = jnp.broadcast_to(
        partial.reshape(bands_total // bands_dev, 1, bands_dev, -1),
        (bands_total // bands_dev, devices // (bands_total // bands_dev), bands_dev, partial.shape[1]),
    ).reshape(devices, bands_dev, partial.shape[1])
    received = lax.all_to_all(per_dest, ("tm", "qband"), 0, 0, tiled=True)
    own = jnp.sum(received, axis=0)
    nlag = lag_list.shape[0]
    target = own[:, :nlag] / (own[:, nlag:] * pixels)

    columns = decay_rates.shape[1]
    ring = lax.axis_size("qband")
    pieces = [decay_rates] + [
        lax.ppermute(decay_rates, "qband", [(j, (j + s) % ring) for j in range(ring)]) for s in range(1, ring)
    ]
    all_rates = jnp.concatenate(pieces, axis=1)
    kernel = kernel_panel(all_rates, lag_list)
    step_size = 1.0 / jnp.sum(kernel * kernel, axis=(1, 2))
    weights = fit_bands(kernel, target, step_size)[:, :columns]
    return (structure, weights)


def solution(mesh):
    placed = (P(("tm", "qband"), None, None), P(), P(("tm", "qband"), None), P("tm", "qband"))
    return jax.shard_map(
        on_device,
        mesh=mesh,
        in_specs=placed,
        out_specs=(P(None, ("tm", "qband"), None), P("tm", "qband")),
        check_vma=False,
    )
```

```python
import math

import jax
import jax.numpy as jnp
from jax import lax
from jax.sharding import PartitionSpec as P
from jax.experimental import pallas as pl
from jax.experimental.pallas import tpu as pltpu

BINS = 1024
ITERS = 64


def dft_table(length):
    positions = jnp.arange(length, dtype=jnp.int32)
    phase_index = positions[:, None] * positions[None, :] % length
    folded = jnp.minimum(phase_index, length - phase_index)
    sign_factor = jnp.where(phase_index * 2 > length, -1.0, 1.0).astype(jnp.float32)
    angles = folded.astype(jnp.float32) * (2.0 * math.pi / length)
    factor = 1.0 / math.sqrt(length)
    return jnp.concatenate(
        [jnp.cos(angles) * factor, -sign_factor * jnp.sin(angles) * factor], axis=1
    ).astype(jnp.bfloat16)


def structure_kernel(lags_ref, x_ref, out_ref, x32_ref):
    frames_all = x_ref.shape[0]
    pixels = out_ref.shape[2]

    def convert(t, carry):
        x32_ref[t] = x_ref[t].astype(jnp.float32)
        return carry

    lax.fori_loop(0, frames_all, convert, 0)

    def one_lag(l, carry):
        lag = lags_ref[l]
        count = frames_all - lag

        def step(t, acc):
            d = x32_ref[t + lag] - x32_ref[t]
            return acc + d * d

        acc = lax.fori_loop(0, count, step, jnp.zeros(x32_ref.shape[1:], jnp.float32))
        out_ref[l] = (acc[:, :pixels] + acc[:, pixels:]) / count.astype(jnp.float32)
        return carry

    lax.fori_loop(0, lags_ref.shape[0], one_lag, 0)


def structure_block(spectrum_block, lag_list):
    frames_all, rows, width = spectrum_block.shape
    nlag = lag_list.shape[0]
    return pl.pallas_call(
        structure_kernel,
        out_shape=jax.ShapeDtypeStruct((nlag, rows, width // 2), jnp.float32),
        in_specs=[
            pl.BlockSpec(memory_space=pltpu.SMEM),
            pl.BlockSpec(memory_space=pltpu.VMEM),
        ],
        out_specs=pl.BlockSpec(memory_space=pltpu.VMEM),
        scratch_shapes=[
            pltpu.VMEM((frames_all, rows, width), jnp.float32),
        ],
        compiler_params=pltpu.CompilerParams(vmem_limit_bytes=40 * 1024 * 1024),
    )(lag_list, spectrum_block)


def kernel_panel(decay_rates, lag_list):
    lag_values = lag_list.astype(jnp.float32)
    return (1.0 - jnp.exp(-decay_rates[:, None, :] * lag_values[None, :, None])) / BINS


def fit_kernel(k_ref, tgt_ref, step_ref, w_ref):
    panel = k_ref[...]
    tgt = tgt_ref[...][:, :, 0:1]
    step = step_ref[...]

    def body(i, w):
        predicted = jnp.sum(panel * w, axis=2, keepdims=True)
        residual = predicted - tgt
        gradient = jnp.sum(panel * residual, axis=1, keepdims=True)
        return jnp.maximum(w - step * gradient, 0.0)

    w_ref[...] = lax.fori_loop(0, ITERS, body, jnp.zeros(step.shape, jnp.float32))


def fit_bands(kernel, target, step_size):
    bands, lags, bins = kernel.shape
    tgt = jnp.broadcast_to(target[:, :, None], (bands, lags, 128))
    step = jnp.broadcast_to(step_size[:, None, None], (bands, 1, bins))
    out = pl.pallas_call(
        fit_kernel,
        out_shape=jax.ShapeDtypeStruct((bands, 1, bins), jnp.float32),
    )(kernel, tgt, step)
    return out[:, 0, :]


def on_device(frames, lag_list, band_index, decay_rates):
    pixels = frames.shape[1]
    devices = lax.axis_size(("tm", "qband"))
    table = lax.optimization_barrier(dft_table(pixels))
    row_transform = jnp.dot(frames[0], table, preferred_element_type=jnp.float32).astype(jnp.bfloat16)
    row_transform = row_transform.reshape(pixels, 2, pixels)
    cos_part = table[:, :pixels]
    sin_part = table[:, pixels:]
    mixing = jnp.stack([table, jnp.concatenate([-sin_part, cos_part], axis=1)])
    spectrum = jnp.einsum("ypk,pyj->kj", row_transform, mixing, preferred_element_type=jnp.float32)
    spectrum = spectrum.astype(jnp.bfloat16).reshape(devices, pixels // devices, 2 * pixels)
    gathered = lax.all_to_all(spectrum, ("tm", "qband"), 0, 0, tiled=True)
    structure = structure_block(gathered, lag_list)

    bands_dev = decay_rates.shape[0]
    bands_total = bands_dev * lax.axis_size("tm")
    row_sums = jnp.sum(structure, axis=2)
    band_ids = jnp.arange(bands_total, dtype=jnp.int32)
    one_hot = (band_index[:, 0][None, :] == band_ids[:, None]).astype(jnp.float32)
    partial_totals = jnp.dot(one_hot, row_sums.T, precision=lax.Precision.HIGHEST)
    partial_counts = jnp.sum(one_hot, axis=1, keepdims=True)
    partial = jnp.concatenate([partial_totals, partial_counts], axis=1)
    per_dest = jnp.broadcast_to(
        partial.reshape(bands_total // bands_dev, 1, bands_dev, -1),
        (bands_total // bands_dev, devices // (bands_total // bands_dev), bands_dev, partial.shape[1]),
    ).reshape(devices, bands_dev, partial.shape[1])
    received = lax.all_to_all(per_dest, ("tm", "qband"), 0, 0, tiled=True)
    own = jnp.sum(received, axis=0)
    nlag = lag_list.shape[0]
    target = own[:, :nlag] / (own[:, nlag:] * pixels)

    columns = decay_rates.shape[1]
    ring = lax.axis_size("qband")
    pieces = [decay_rates] + [
        lax.ppermute(decay_rates, "qband", [(j, (j + s) % ring) for j in range(ring)]) for s in range(1, ring)
    ]
    all_rates = jnp.concatenate(pieces, axis=1)
    kernel = kernel_panel(all_rates, lag_list)
    step_size = 1.0 / jnp.sum(kernel * kernel, axis=(1, 2))
    weights = fit_bands(kernel, target, step_size)[:, :columns]
    return (structure, weights)


def solution(mesh):
    placed = (P(("tm", "qband"), None, None), P(), P(("tm", "qband"), None), P("tm", "qband"))
    return jax.shard_map(
        on_device,
        mesh=mesh,
        in_specs=placed,
        out_specs=(P(None, ("tm", "qband"), None), P("tm", "qband")),
        check_vma=False,
    )
```

```python
import math

import jax
import jax.numpy as jnp
from jax import lax
from jax.sharding import PartitionSpec as P
from jax.experimental import pallas as pl
from jax.experimental.pallas import tpu as pltpu

BINS = 1024
ITERS = 64
CHUNKS = 4


def dft_table(length):
    positions = jnp.arange(length, dtype=jnp.int32)
    phase_index = positions[:, None] * positions[None, :] % length
    folded = jnp.minimum(phase_index, length - phase_index)
    sign_factor = jnp.where(phase_index * 2 > length, -1.0, 1.0).astype(jnp.float32)
    angles = folded.astype(jnp.float32) * (2.0 * math.pi / length)
    factor = 1.0 / math.sqrt(length)
    return jnp.concatenate(
        [jnp.cos(angles) * factor, -sign_factor * jnp.sin(angles) * factor], axis=1
    ).astype(jnp.bfloat16)


def structure_kernel(lags_ref, x_ref, out_ref, x32_ref):
    frames_all = x_ref.shape[0]
    pixels = out_ref.shape[2]

    def convert(t, carry):
        x32_ref[t] = x_ref[t].astype(jnp.float32)
        return carry

    lax.fori_loop(0, frames_all, convert, 0)

    def one_lag(l, carry):
        lag = lags_ref[l]
        count = frames_all - lag

        def step(t, acc):
            d = x32_ref[t + lag] - x32_ref[t]
            return acc + d * d

        acc = lax.fori_loop(0, count, step, jnp.zeros(x32_ref.shape[1:], jnp.float32))
        out_ref[l] = (acc[:, :pixels] + acc[:, pixels:]) / count.astype(jnp.float32)
        return carry

    lax.fori_loop(0, lags_ref.shape[0], one_lag, 0)


def structure_block(spectrum_block, lag_list):
    frames_all, rows, width = spectrum_block.shape
    nlag = lag_list.shape[0]
    return pl.pallas_call(
        structure_kernel,
        out_shape=jax.ShapeDtypeStruct((nlag, rows, width // 2), jnp.float32),
        in_specs=[
            pl.BlockSpec(memory_space=pltpu.SMEM),
            pl.BlockSpec(memory_space=pltpu.VMEM),
        ],
        out_specs=pl.BlockSpec(memory_space=pltpu.VMEM),
        scratch_shapes=[
            pltpu.VMEM((frames_all, rows, width), jnp.float32),
        ],
        compiler_params=pltpu.CompilerParams(vmem_limit_bytes=40 * 1024 * 1024),
    )(lag_list, spectrum_block)


def kernel_panel(decay_rates, lag_list):
    lag_values = lag_list.astype(jnp.float32)
    return (1.0 - jnp.exp(-decay_rates[:, None, :] * lag_values[None, :, None])) / BINS


def fit_kernel(k_ref, tgt_ref, step_ref, w_ref):
    panel = k_ref[...]
    tgt = tgt_ref[...][:, :, 0:1]
    step = step_ref[...]

    def body(i, w):
        predicted = jnp.sum(panel * w, axis=2, keepdims=True)
        residual = predicted - tgt
        gradient = jnp.sum(panel * residual, axis=1, keepdims=True)
        return jnp.maximum(w - step * gradient, 0.0)

    w_ref[...] = lax.fori_loop(0, ITERS, body, jnp.zeros(step.shape, jnp.float32))


def fit_bands(kernel, target, step_size):
    bands, lags, bins = kernel.shape
    tgt = jnp.broadcast_to(target[:, :, None], (bands, lags, 128))
    step = jnp.broadcast_to(step_size[:, None, None], (bands, 1, bins))
    out = pl.pallas_call(
        fit_kernel,
        out_shape=jax.ShapeDtypeStruct((bands, 1, bins), jnp.float32),
    )(kernel, tgt, step)
    return out[:, 0, :]


def on_device(frames, lag_list, band_index, decay_rates):
    pixels = frames.shape[1]
    devices = lax.axis_size(("tm", "qband"))
    table = lax.optimization_barrier(dft_table(pixels))
    row_transform = jnp.dot(frames[0], table, preferred_element_type=jnp.float32).astype(jnp.bfloat16)
    row_transform = row_transform.reshape(pixels, 2, pixels)
    cos_part = table[:, :pixels]
    sin_part = table[:, pixels:]
    width = pixels // CHUNKS
    pieces_out = []
    for k in range(CHUNKS):
        cols = slice(k * width, (k + 1) * width)
        mixing = jnp.stack([
            jnp.concatenate([cos_part[:, cols], sin_part[:, cols]], axis=1),
            jnp.concatenate([-sin_part[:, cols], cos_part[:, cols]], axis=1),
        ])
        spectrum = jnp.einsum("ypk,pyj->kj", row_transform, mixing, preferred_element_type=jnp.float32)
        spectrum = spectrum.astype(jnp.bfloat16).reshape(devices, pixels // devices, 2 * width)
        gathered = lax.all_to_all(spectrum, ("tm", "qband"), 0, 0, tiled=True)
        pieces_out.append(structure_block(gathered, lag_list))
    structure = jnp.concatenate(pieces_out, axis=2)

    bands_dev = decay_rates.shape[0]
    bands_total = bands_dev * lax.axis_size("tm")
    row_sums = jnp.sum(structure, axis=2)
    band_ids = jnp.arange(bands_total, dtype=jnp.int32)
    one_hot = (band_index[:, 0][None, :] == band_ids[:, None]).astype(jnp.float32)
    partial_totals = jnp.dot(one_hot, row_sums.T, precision=lax.Precision.HIGHEST)
    partial_counts = jnp.sum(one_hot, axis=1, keepdims=True)
    partial = jnp.concatenate([partial_totals, partial_counts], axis=1)
    per_dest = jnp.broadcast_to(
        partial.reshape(bands_total // bands_dev, 1, bands_dev, -1),
        (bands_total // bands_dev, devices // (bands_total // bands_dev), bands_dev, partial.shape[1]),
    ).reshape(devices, bands_dev, partial.shape[1])
    received = lax.all_to_all(per_dest, ("tm", "qband"), 0, 0, tiled=True)
    own = jnp.sum(received, axis=0)
    nlag = lag_list.shape[0]
    target = own[:, :nlag] / (own[:, nlag:] * pixels)

    columns = decay_rates.shape[1]
    ring = lax.axis_size("qband")
    pieces = [decay_rates] + [
        lax.ppermute(decay_rates, "qband", [(j, (j + s) % ring) for j in range(ring)]) for s in range(1, ring)
    ]
    all_rates = jnp.concatenate(pieces, axis=1)
    kernel = kernel_panel(all_rates, lag_list)
    step_size = 1.0 / jnp.sum(kernel * kernel, axis=(1, 2))
    weights = fit_bands(kernel, target, step_size)[:, :columns]
    return (structure, weights)


def solution(mesh):
    placed = (P(("tm", "qband"), None, None), P(), P(("tm", "qband"), None), P("tm", "qband"))
    return jax.shard_map(
        on_device,
        mesh=mesh,
        in_specs=placed,
        out_specs=(P(None, ("tm", "qband"), None), P("tm", "qband")),
        check_vma=False,
    )
```

```python
import math

import jax
import jax.numpy as jnp
from jax import lax
from jax.sharding import PartitionSpec as P
from jax.experimental import pallas as pl
from jax.experimental.pallas import tpu as pltpu

BINS = 1024
ITERS = 64
CHUNKS = 1
UNROLL = 4


def dft_table(length):
    positions = jnp.arange(length, dtype=jnp.int32)
    phase_index = positions[:, None] * positions[None, :] % length
    folded = jnp.minimum(phase_index, length - phase_index)
    sign_factor = jnp.where(phase_index * 2 > length, -1.0, 1.0).astype(jnp.float32)
    angles = folded.astype(jnp.float32) * (2.0 * math.pi / length)
    factor = 1.0 / math.sqrt(length)
    return jnp.concatenate(
        [jnp.cos(angles) * factor, -sign_factor * jnp.sin(angles) * factor], axis=1
    ).astype(jnp.bfloat16)


def structure_kernel(lags_ref, x_ref, out_ref, x32_ref):
    frames_all = x_ref.shape[0]
    pixels = out_ref.shape[2]

    def convert(t, carry):
        x32_ref[t] = x_ref[t].astype(jnp.float32)
        return carry

    lax.fori_loop(0, frames_all, convert, 0)

    def one_lag(l, carry):
        lag = lags_ref[l]
        count = frames_all - lag

        def step(t, acc):
            d = x32_ref[t + lag] - x32_ref[t]
            return acc + d * d

        def step_block(i, acc):
            for u in range(UNROLL):
                acc = step(i * UNROLL + u, acc)
            return acc

        blocks = count // UNROLL
        acc = lax.fori_loop(0, blocks, step_block, jnp.zeros(x32_ref.shape[1:], jnp.float32))
        acc = lax.fori_loop(blocks * UNROLL, count, step, acc)
        out_ref[l] = (acc[:, :pixels] + acc[:, pixels:]) / count.astype(jnp.float32)
        return carry

    lax.fori_loop(0, lags_ref.shape[0], one_lag, 0)


def structure_block(spectrum_block, lag_list):
    frames_all, rows, width = spectrum_block.shape
    nlag = lag_list.shape[0]
    return pl.pallas_call(
        structure_kernel,
        out_shape=jax.ShapeDtypeStruct((nlag, rows, width // 2), jnp.float32),
        in_specs=[
            pl.BlockSpec(memory_space=pltpu.SMEM),
            pl.BlockSpec(memory_space=pltpu.VMEM),
        ],
        out_specs=pl.BlockSpec(memory_space=pltpu.VMEM),
        scratch_shapes=[
            pltpu.VMEM((frames_all, rows, width), jnp.float32),
        ],
        compiler_params=pltpu.CompilerParams(vmem_limit_bytes=40 * 1024 * 1024),
    )(lag_list, spectrum_block)


def kernel_panel(decay_rates, lag_list):
    lag_values = lag_list.astype(jnp.float32)
    return (1.0 - jnp.exp(-decay_rates[:, None, :] * lag_values[None, :, None])) / BINS


def fit_kernel(k_ref, tgt_ref, step_ref, w_ref):
    panel = k_ref[...]
    tgt = tgt_ref[...][:, :, 0:1]
    step = step_ref[...]

    def body(i, w):
        predicted = jnp.sum(panel * w, axis=2, keepdims=True)
        residual = predicted - tgt
        gradient = jnp.sum(panel * residual, axis=1, keepdims=True)
        return jnp.maximum(w - step * gradient, 0.0)

    w_ref[...] = lax.fori_loop(0, ITERS, body, jnp.zeros(step.shape, jnp.float32))


def fit_bands(kernel, target, step_size):
    bands, lags, bins = kernel.shape
    tgt = jnp.broadcast_to(target[:, :, None], (bands, lags, 128))
    step = jnp.broadcast_to(step_size[:, None, None], (bands, 1, bins))
    out = pl.pallas_call(
        fit_kernel,
        out_shape=jax.ShapeDtypeStruct((bands, 1, bins), jnp.float32),
    )(kernel, tgt, step)
    return out[:, 0, :]


def on_device(frames, lag_list, band_index, decay_rates):
    pixels = frames.shape[1]
    devices = lax.axis_size(("tm", "qband"))
    table = lax.optimization_barrier(dft_table(pixels))
    row_transform = jnp.dot(frames[0], table, preferred_element_type=jnp.float32).astype(jnp.bfloat16)
    row_transform = row_transform.reshape(pixels, 2, pixels)
    cos_part = table[:, :pixels]
    sin_part = table[:, pixels:]
    width = pixels // CHUNKS
    pieces_out = []
    for k in range(CHUNKS):
        cols = slice(k * width, (k + 1) * width)
        mixing = jnp.stack([
            jnp.concatenate([cos_part[:, cols], sin_part[:, cols]], axis=1),
            jnp.concatenate([-sin_part[:, cols], cos_part[:, cols]], axis=1),
        ])
        spectrum = jnp.einsum("ypk,pyj->kj", row_transform, mixing, preferred_element_type=jnp.float32)
        spectrum = spectrum.astype(jnp.bfloat16).reshape(devices, pixels // devices, 2 * width)
        gathered = lax.all_to_all(spectrum, ("tm", "qband"), 0, 0, tiled=True)
        pieces_out.append(structure_block(gathered, lag_list))
    structure = jnp.concatenate(pieces_out, axis=2)

    bands_dev = decay_rates.shape[0]
    bands_total = bands_dev * lax.axis_size("tm")
    row_sums = jnp.sum(structure, axis=2)
    band_ids = jnp.arange(bands_total, dtype=jnp.int32)
    one_hot = (band_index[:, 0][None, :] == band_ids[:, None]).astype(jnp.float32)
    partial_totals = jnp.dot(one_hot, row_sums.T, precision=lax.Precision.HIGHEST)
    partial_counts = jnp.sum(one_hot, axis=1, keepdims=True)
    partial = jnp.concatenate([partial_totals, partial_counts], axis=1)
    per_dest = jnp.broadcast_to(
        partial.reshape(bands_total // bands_dev, 1, bands_dev, -1),
        (bands_total // bands_dev, devices // (bands_total // bands_dev), bands_dev, partial.shape[1]),
    ).reshape(devices, bands_dev, partial.shape[1])
    received = lax.all_to_all(per_dest, ("tm", "qband"), 0, 0, tiled=True)
    own = jnp.sum(received, axis=0)
    nlag = lag_list.shape[0]
    target = own[:, :nlag] / (own[:, nlag:] * pixels)

    columns = decay_rates.shape[1]
    ring = lax.axis_size("qband")
    pieces = [decay_rates] + [
        lax.ppermute(decay_rates, "qband", [(j, (j + s) % ring) for j in range(ring)]) for s in range(1, ring)
    ]
    all_rates = jnp.concatenate(pieces, axis=1)
    kernel = kernel_panel(all_rates, lag_list)
    step_size = 1.0 / jnp.sum(kernel * kernel, axis=(1, 2))
    weights = fit_bands(kernel, target, step_size)[:, :columns]
    return (structure, weights)


def solution(mesh):
    placed = (P(("tm", "qband"), None, None), P(), P(("tm", "qband"), None), P("tm", "qband"))
    return jax.shard_map(
        on_device,
        mesh=mesh,
        in_specs=placed,
        out_specs=(P(None, ("tm", "qband"), None), P("tm", "qband")),
        check_vma=False,
    )
```

```python
import math

import jax
import jax.numpy as jnp
from jax import lax
from jax.sharding import PartitionSpec as P
from jax.experimental import pallas as pl
from jax.experimental.pallas import tpu as pltpu

BINS = 1024
ITERS = 64
CHUNKS = 1
UNROLL = 8


def dft_table(length):
    positions = jnp.arange(length, dtype=jnp.int32)
    phase_index = positions[:, None] * positions[None, :] % length
    folded = jnp.minimum(phase_index, length - phase_index)
    sign_factor = jnp.where(phase_index * 2 > length, -1.0, 1.0).astype(jnp.float32)
    angles = folded.astype(jnp.float32) * (2.0 * math.pi / length)
    factor = 1.0 / math.sqrt(length)
    return jnp.concatenate(
        [jnp.cos(angles) * factor, -sign_factor * jnp.sin(angles) * factor], axis=1
    ).astype(jnp.bfloat16)


def structure_kernel(lags_ref, x_ref, out_ref, x32_ref):
    frames_all = x_ref.shape[0]
    pixels = out_ref.shape[2]

    def convert(t, carry):
        x32_ref[t] = x_ref[t].astype(jnp.float32)
        return carry

    lax.fori_loop(0, frames_all, convert, 0)

    def one_lag(l, carry):
        lag = lags_ref[l]
        count = frames_all - lag

        def step(t, acc):
            d = x32_ref[t + lag] - x32_ref[t]
            return acc + d * d

        def step_block(i, acc):
            for u in range(UNROLL):
                acc = step(i * UNROLL + u, acc)
            return acc

        blocks = count // UNROLL
        acc = lax.fori_loop(0, blocks, step_block, jnp.zeros(x32_ref.shape[1:], jnp.float32))
        acc = lax.fori_loop(blocks * UNROLL, count, step, acc)
        out_ref[l] = (acc[:, :pixels] + acc[:, pixels:]) / count.astype(jnp.float32)
        return carry

    lax.fori_loop(0, lags_ref.shape[0], one_lag, 0)


def structure_block(spectrum_block, lag_list):
    frames_all, rows, width = spectrum_block.shape
    nlag = lag_list.shape[0]
    return pl.pallas_call(
        structure_kernel,
        out_shape=jax.ShapeDtypeStruct((nlag, rows, width // 2), jnp.float32),
        in_specs=[
            pl.BlockSpec(memory_space=pltpu.SMEM),
            pl.BlockSpec(memory_space=pltpu.VMEM),
        ],
        out_specs=pl.BlockSpec(memory_space=pltpu.VMEM),
        scratch_shapes=[
            pltpu.VMEM((frames_all, rows, width), jnp.float32),
        ],
        compiler_params=pltpu.CompilerParams(vmem_limit_bytes=40 * 1024 * 1024),
    )(lag_list, spectrum_block)


def kernel_panel(decay_rates, lag_list):
    lag_values = lag_list.astype(jnp.float32)
    return (1.0 - jnp.exp(-decay_rates[:, None, :] * lag_values[None, :, None])) / BINS


def fit_kernel(k_ref, tgt_ref, step_ref, w_ref):
    panel = k_ref[...]
    tgt = tgt_ref[...][:, :, 0:1]
    step = step_ref[...]

    def body(i, w):
        predicted = jnp.sum(panel * w, axis=2, keepdims=True)
        residual = predicted - tgt
        gradient = jnp.sum(panel * residual, axis=1, keepdims=True)
        return jnp.maximum(w - step * gradient, 0.0)

    w_ref[...] = lax.fori_loop(0, ITERS, body, jnp.zeros(step.shape, jnp.float32), unroll=4)


def fit_bands(kernel, target, step_size):
    bands, lags, bins = kernel.shape
    tgt = jnp.broadcast_to(target[:, :, None], (bands, lags, 128))
    step = jnp.broadcast_to(step_size[:, None, None], (bands, 1, bins))
    out = pl.pallas_call(
        fit_kernel,
        out_shape=jax.ShapeDtypeStruct((bands, 1, bins), jnp.float32),
    )(kernel, tgt, step)
    return out[:, 0, :]


def on_device(frames, lag_list, band_index, decay_rates):
    pixels = frames.shape[1]
    devices = lax.axis_size(("tm", "qband"))
    table = lax.optimization_barrier(dft_table(pixels))
    row_transform = jnp.dot(frames[0], table, preferred_element_type=jnp.float32).astype(jnp.bfloat16)
    row_transform = row_transform.reshape(pixels, 2, pixels)
    cos_part = table[:, :pixels]
    sin_part = table[:, pixels:]
    width = pixels // CHUNKS
    pieces_out = []
    for k in range(CHUNKS):
        cols = slice(k * width, (k + 1) * width)
        mixing = jnp.stack([
            jnp.concatenate([cos_part[:, cols], sin_part[:, cols]], axis=1),
            jnp.concatenate([-sin_part[:, cols], cos_part[:, cols]], axis=1),
        ])
        spectrum = jnp.einsum("ypk,pyj->kj", row_transform, mixing, preferred_element_type=jnp.float32)
        spectrum = spectrum.astype(jnp.bfloat16).reshape(devices, pixels // devices, 2 * width)
        gathered = lax.all_to_all(spectrum, ("tm", "qband"), 0, 0, tiled=True)
        pieces_out.append(structure_block(gathered, lag_list))
    structure = jnp.concatenate(pieces_out, axis=2)

    bands_dev = decay_rates.shape[0]
    bands_total = bands_dev * lax.axis_size("tm")
    row_sums = jnp.sum(structure, axis=2)
    band_ids = jnp.arange(bands_total, dtype=jnp.int32)
    one_hot = (band_index[:, 0][None, :] == band_ids[:, None]).astype(jnp.float32)
    partial_totals = jnp.dot(one_hot, row_sums.T, precision=lax.Precision.HIGHEST)
    partial_counts = jnp.sum(one_hot, axis=1, keepdims=True)
    partial = jnp.concatenate([partial_totals, partial_counts], axis=1)
    per_dest = jnp.broadcast_to(
        partial.reshape(bands_total // bands_dev, 1, bands_dev, -1),
        (bands_total // bands_dev, devices // (bands_total // bands_dev), bands_dev, partial.shape[1]),
    ).reshape(devices, bands_dev, partial.shape[1])
    received = lax.all_to_all(per_dest, ("tm", "qband"), 0, 0, tiled=True)
    own = jnp.sum(received, axis=0)
    nlag = lag_list.shape[0]
    target = own[:, :nlag] / (own[:, nlag:] * pixels)

    columns = decay_rates.shape[1]
    ring = lax.axis_size("qband")
    pieces = [decay_rates] + [
        lax.ppermute(decay_rates, "qband", [(j, (j + s) % ring) for j in range(ring)]) for s in range(1, ring)
    ]
    all_rates = jnp.concatenate(pieces, axis=1)
    kernel = kernel_panel(all_rates, lag_list)
    step_size = 1.0 / jnp.sum(kernel * kernel, axis=(1, 2))
    weights = fit_bands(kernel, target, step_size)[:, :columns]
    return (structure, weights)


def solution(mesh):
    placed = (P(("tm", "qband"), None, None), P(), P(("tm", "qband"), None), P("tm", "qband"))
    return jax.shard_map(
        on_device,
        mesh=mesh,
        in_specs=placed,
        out_specs=(P(None, ("tm", "qband"), None), P("tm", "qband")),
        check_vma=False,
    )
```

```python
import math

import jax
import jax.numpy as jnp
from jax import lax
from jax.sharding import PartitionSpec as P
from jax.experimental import pallas as pl
from jax.experimental.pallas import tpu as pltpu

BINS = 1024
ITERS = 64
CHUNKS = 1
UNROLL = 8


def dft_table(length):
    positions = jnp.arange(length, dtype=jnp.int32)
    phase_index = positions[:, None] * positions[None, :] % length
    folded = jnp.minimum(phase_index, length - phase_index)
    sign_factor = jnp.where(phase_index * 2 > length, -1.0, 1.0).astype(jnp.float32)
    angles = folded.astype(jnp.float32) * (2.0 * math.pi / length)
    factor = 1.0 / math.sqrt(length)
    return jnp.concatenate(
        [jnp.cos(angles) * factor, -sign_factor * jnp.sin(angles) * factor], axis=1
    ).astype(jnp.bfloat16)


def structure_kernel(lags_ref, x_ref, out_ref, x32_ref):
    frames_all = x_ref.shape[0]
    pixels = out_ref.shape[2]

    def convert(t, carry):
        x32_ref[t] = x_ref[t].astype(jnp.float32)
        return carry

    lax.fori_loop(0, frames_all, convert, 0)

    def one_lag(l, carry):
        lag = lags_ref[l]
        count = frames_all - lag

        def step(t, acc):
            d = x32_ref[t + lag] - x32_ref[t]
            return acc + d * d

        def step_block(i, acc):
            for u in range(UNROLL):
                acc = step(i * UNROLL + u, acc)
            return acc

        blocks = count // UNROLL
        acc = lax.fori_loop(0, blocks, step_block, jnp.zeros(x32_ref.shape[1:], jnp.float32))
        acc = lax.fori_loop(blocks * UNROLL, count, step, acc)
        out_ref[l] = (acc[:, :pixels] + acc[:, pixels:]) / count.astype(jnp.float32)
        return carry

    lax.fori_loop(0, lags_ref.shape[0], one_lag, 0)


def structure_block(spectrum_block, lag_list):
    frames_all, rows, width = spectrum_block.shape
    nlag = lag_list.shape[0]
    return pl.pallas_call(
        structure_kernel,
        out_shape=jax.ShapeDtypeStruct((nlag, rows, width // 2), jnp.float32),
        in_specs=[
            pl.BlockSpec(memory_space=pltpu.SMEM),
            pl.BlockSpec(memory_space=pltpu.VMEM),
        ],
        out_specs=pl.BlockSpec(memory_space=pltpu.VMEM),
        scratch_shapes=[
            pltpu.VMEM((frames_all, rows, width), jnp.float32),
        ],
        compiler_params=pltpu.CompilerParams(vmem_limit_bytes=40 * 1024 * 1024),
    )(lag_list, spectrum_block)


def table_columns(length, first, count):
    rows = jnp.arange(length, dtype=jnp.int32)
    cols = jnp.arange(count, dtype=jnp.int32) + first
    phase_index = rows[:, None] * cols[None, :] % length
    folded = jnp.minimum(phase_index, length - phase_index)
    sign_factor = jnp.where(phase_index * 2 > length, -1.0, 1.0).astype(jnp.float32)
    angles = folded.astype(jnp.float32) * (2.0 * math.pi / length)
    factor = 1.0 / math.sqrt(length)
    return jnp.stack([jnp.cos(angles) * factor, -sign_factor * jnp.sin(angles) * factor]).astype(jnp.bfloat16)


def shared_table(length):
    ring = lax.axis_size("qband")
    core = lax.axis_index("qband") % 2
    half = length // 2
    mine = table_columns(length, core * half, half)
    other = lax.ppermute(mine, "qband", [(j, j ^ 1) for j in range(ring)])
    first = jnp.where(core == 0, mine, other)
    second = jnp.where(core == 0, other, mine)
    both = jnp.concatenate([first, second], axis=2)
    return jnp.concatenate([both[0], both[1]], axis=1)


def kernel_panel(decay_rates, lag_list):
    lag_values = lag_list.astype(jnp.float32)
    return (1.0 - jnp.exp(-decay_rates[:, None, :] * lag_values[None, :, None])) / BINS


def fit_kernel(k_ref, tgt_ref, step_ref, w_ref):
    panel = k_ref[...]
    tgt = tgt_ref[...][:, :, 0:1]
    step = step_ref[...]

    def body(i, w):
        predicted = jnp.sum(panel * w, axis=2, keepdims=True)
        residual = predicted - tgt
        gradient = jnp.sum(panel * residual, axis=1, keepdims=True)
        return jnp.maximum(w - step * gradient, 0.0)

    w_ref[...] = lax.fori_loop(0, ITERS, body, jnp.zeros(step.shape, jnp.float32), unroll=4)


def fit_bands(kernel, target, step_size):
    bands, lags, bins = kernel.shape
    tgt = jnp.broadcast_to(target[:, :, None], (bands, lags, 128))
    step = jnp.broadcast_to(step_size[:, None, None], (bands, 1, bins))
    out = pl.pallas_call(
        fit_kernel,
        out_shape=jax.ShapeDtypeStruct((bands, 1, bins), jnp.float32),
    )(kernel, tgt, step)
    return out[:, 0, :]


def on_device(frames, lag_list, band_index, decay_rates):
    pixels = frames.shape[1]
    devices = lax.axis_size(("tm", "qband"))
    table = lax.optimization_barrier(shared_table(pixels))
    row_transform = jnp.dot(frames[0], table, preferred_element_type=jnp.float32).astype(jnp.bfloat16)
    row_transform = row_transform.reshape(pixels, 2, pixels)
    cos_part = table[:, :pixels]
    sin_part = table[:, pixels:]
    width = pixels // CHUNKS
    pieces_out = []
    for k in range(CHUNKS):
        cols = slice(k * width, (k + 1) * width)
        mixing = jnp.stack([
            jnp.concatenate([cos_part[:, cols], sin_part[:, cols]], axis=1),
            jnp.concatenate([-sin_part[:, cols], cos_part[:, cols]], axis=1),
        ])
        spectrum = jnp.einsum("ypk,pyj->kj", row_transform, mixing, preferred_element_type=jnp.float32)
        spectrum = spectrum.astype(jnp.bfloat16).reshape(devices, pixels // devices, 2 * width)
        gathered = lax.all_to_all(spectrum, ("tm", "qband"), 0, 0, tiled=True)
        pieces_out.append(structure_block(gathered, lag_list))
    structure = jnp.concatenate(pieces_out, axis=2)

    bands_dev = decay_rates.shape[0]
    bands_total = bands_dev * lax.axis_size("tm")
    row_sums = jnp.sum(structure, axis=2)
    band_ids = jnp.arange(bands_total, dtype=jnp.int32)
    one_hot = (band_index[:, 0][None, :] == band_ids[:, None]).astype(jnp.float32)
    partial_totals = jnp.dot(one_hot, row_sums.T, precision=lax.Precision.HIGHEST)
    partial_counts = jnp.sum(one_hot, axis=1, keepdims=True)
    partial = jnp.concatenate([partial_totals, partial_counts], axis=1)
    per_dest = jnp.broadcast_to(
        partial.reshape(bands_total // bands_dev, 1, bands_dev, -1),
        (bands_total // bands_dev, devices // (bands_total // bands_dev), bands_dev, partial.shape[1]),
    ).reshape(devices, bands_dev, partial.shape[1])
    received = lax.all_to_all(per_dest, ("tm", "qband"), 0, 0, tiled=True)
    own = jnp.sum(received, axis=0)
    nlag = lag_list.shape[0]
    target = own[:, :nlag] / (own[:, nlag:] * pixels)

    columns = decay_rates.shape[1]
    ring = lax.axis_size("qband")
    pieces = [decay_rates] + [
        lax.ppermute(decay_rates, "qband", [(j, (j + s) % ring) for j in range(ring)]) for s in range(1, ring)
    ]
    all_rates = jnp.concatenate(pieces, axis=1)
    kernel = kernel_panel(all_rates, lag_list)
    step_size = 1.0 / jnp.sum(kernel * kernel, axis=(1, 2))
    weights = fit_bands(kernel, target, step_size)[:, :columns]
    return (structure, weights)


def solution(mesh):
    placed = (P(("tm", "qband"), None, None), P(), P(("tm", "qband"), None), P("tm", "qband"))
    return jax.shard_map(
        on_device,
        mesh=mesh,
        in_specs=placed,
        out_specs=(P(None, ("tm", "qband"), None), P("tm", "qband")),
        check_vma=False,
    )
```

```python
import math

import jax
import jax.numpy as jnp
from jax import lax
from jax.sharding import PartitionSpec as P
from jax.experimental import pallas as pl
from jax.experimental.pallas import tpu as pltpu

BINS = 1024
ITERS = 64
CHUNKS = 1
UNROLL = 8


def dft_table(length):
    positions = jnp.arange(length, dtype=jnp.int32)
    phase_index = positions[:, None] * positions[None, :] % length
    folded = jnp.minimum(phase_index, length - phase_index)
    sign_factor = jnp.where(phase_index * 2 > length, -1.0, 1.0).astype(jnp.float32)
    angles = folded.astype(jnp.float32) * (2.0 * math.pi / length)
    factor = 1.0 / math.sqrt(length)
    return jnp.concatenate(
        [jnp.cos(angles) * factor, -sign_factor * jnp.sin(angles) * factor], axis=1
    ).astype(jnp.bfloat16)


def structure_kernel(lags_ref, x_ref, out_ref, x32_ref):
    frames_all = x_ref.shape[0]
    pixels = out_ref.shape[2]

    def convert(t, carry):
        x32_ref[t] = x_ref[t].astype(jnp.float32)
        return carry

    lax.fori_loop(0, frames_all, convert, 0)

    def one_lag(l, carry):
        lag = lags_ref[l]
        count = frames_all - lag

        def step(t, acc):
            d = x32_ref[t + lag] - x32_ref[t]
            return acc + d * d

        def step_block(i, acc):
            for u in range(UNROLL):
                acc = step(i * UNROLL + u, acc)
            return acc

        blocks = count // UNROLL
        acc = lax.fori_loop(0, blocks, step_block, jnp.zeros(x32_ref.shape[1:], jnp.float32))
        acc = lax.fori_loop(blocks * UNROLL, count, step, acc)
        out_ref[l] = (acc[:, :pixels] + acc[:, pixels:]) / count.astype(jnp.float32)
        return carry

    lax.fori_loop(0, lags_ref.shape[0], one_lag, 0)


def structure_block(spectrum_block, lag_list):
    frames_all, rows, width = spectrum_block.shape
    nlag = lag_list.shape[0]
    return pl.pallas_call(
        structure_kernel,
        out_shape=jax.ShapeDtypeStruct((nlag, rows, width // 2), jnp.float32),
        in_specs=[
            pl.BlockSpec(memory_space=pltpu.SMEM),
            pl.BlockSpec(memory_space=pltpu.VMEM),
        ],
        out_specs=pl.BlockSpec(memory_space=pltpu.VMEM),
        scratch_shapes=[
            pltpu.VMEM((frames_all, rows, width), jnp.float32),
        ],
        compiler_params=pltpu.CompilerParams(vmem_limit_bytes=40 * 1024 * 1024),
    )(lag_list, spectrum_block)


def kernel_panel(decay_rates, lag_list):
    lag_values = lag_list.astype(jnp.float32)
    return (1.0 - jnp.exp(-decay_rates[:, None, :] * lag_values[None, :, None])) / BINS


def fit_kernel(k_ref, tgt_ref, step_ref, w_ref):
    bands, lags, bins = k_ref.shape
    halves = lags // 8
    tiles = bins // 128

    def lane_total(x):
        shift = 64
        while shift >= 1:
            x = x + pltpu.roll(x, shift, 1)
            shift //= 2
        return x

    def sublane_total(x):
        shift = 4
        while shift >= 1:
            x = x + pltpu.roll(x, shift, 0)
            shift //= 2
        return x

    def body(it, w):
        new_w = []
        for b in range(bands):
            residual = []
            for h in range(halves):
                acc = None
                for i in range(tiles):
                    term = k_ref[b, h * 8:(h + 1) * 8, i * 128:(i + 1) * 128] * w[b * tiles + i]
                    acc = term if acc is None else acc + term
                residual.append(lane_total(acc) - tgt_ref[b, h * 8:(h + 1) * 8, :])
            step = step_ref[b]
            for i in range(tiles):
                g = None
                for h in range(halves):
                    term = k_ref[b, h * 8:(h + 1) * 8, i * 128:(i + 1) * 128] * residual[h]
                    g = term if g is None else g + term
                new_w.append(jnp.maximum(w[b * tiles + i] - step * sublane_total(g), 0.0))
        return tuple(new_w)

    init = tuple(jnp.zeros((8, 128), jnp.float32) for _ in range(bands * tiles))
    w = lax.fori_loop(0, ITERS, body, init)
    for b in range(bands):
        for i in range(tiles):
            w_ref[b, :, i * 128:(i + 1) * 128] = w[b * tiles + i]


def fit_bands(kernel, target, step_size):
    bands, lags, bins = kernel.shape
    tgt = jnp.broadcast_to(target[:, :, None], (bands, lags, 128))
    step = jnp.broadcast_to(step_size[:, None, None], (bands, 8, 128))
    out = pl.pallas_call(
        fit_kernel,
        out_shape=jax.ShapeDtypeStruct((bands, 8, bins), jnp.float32),
    )(kernel, tgt, step)
    return out[:, 0, :]


def on_device(frames, lag_list, band_index, decay_rates):
    pixels = frames.shape[1]
    devices = lax.axis_size(("tm", "qband"))
    table = lax.optimization_barrier(dft_table(pixels))
    row_transform = jnp.dot(frames[0], table, preferred_element_type=jnp.float32).astype(jnp.bfloat16)
    row_transform = row_transform.reshape(pixels, 2, pixels)
    cos_part = table[:, :pixels]
    sin_part = table[:, pixels:]
    width = pixels // CHUNKS
    pieces_out = []
    for k in range(CHUNKS):
        cols = slice(k * width, (k + 1) * width)
        mixing = jnp.stack([
            jnp.concatenate([cos_part[:, cols], sin_part[:, cols]], axis=1),
            jnp.concatenate([-sin_part[:, cols], cos_part[:, cols]], axis=1),
        ])
        spectrum = jnp.einsum("ypk,pyj->kj", row_transform, mixing, preferred_element_type=jnp.float32)
        spectrum = spectrum.astype(jnp.bfloat16).reshape(devices, pixels // devices, 2 * width)
        gathered = lax.all_to_all(spectrum, ("tm", "qband"), 0, 0, tiled=True)
        pieces_out.append(structure_block(gathered, lag_list))
    structure = jnp.concatenate(pieces_out, axis=2)

    bands_dev = decay_rates.shape[0]
    bands_total = bands_dev * lax.axis_size("tm")
    row_sums = jnp.sum(structure, axis=2)
    band_ids = jnp.arange(bands_total, dtype=jnp.int32)
    one_hot = (band_index[:, 0][None, :] == band_ids[:, None]).astype(jnp.float32)
    partial_totals = jnp.dot(one_hot, row_sums.T, precision=lax.Precision.HIGHEST)
    partial_counts = jnp.sum(one_hot, axis=1, keepdims=True)
    partial = jnp.concatenate([partial_totals, partial_counts], axis=1)
    per_dest = jnp.broadcast_to(
        partial.reshape(bands_total // bands_dev, 1, bands_dev, -1),
        (bands_total // bands_dev, devices // (bands_total // bands_dev), bands_dev, partial.shape[1]),
    ).reshape(devices, bands_dev, partial.shape[1])
    received = lax.all_to_all(per_dest, ("tm", "qband"), 0, 0, tiled=True)
    own = jnp.sum(received, axis=0)
    nlag = lag_list.shape[0]
    target = own[:, :nlag] / (own[:, nlag:] * pixels)

    columns = decay_rates.shape[1]
    ring = lax.axis_size("qband")
    pieces = [decay_rates] + [
        lax.ppermute(decay_rates, "qband", [(j, (j + s) % ring) for j in range(ring)]) for s in range(1, ring)
    ]
    all_rates = jnp.concatenate(pieces, axis=1)
    kernel = kernel_panel(all_rates, lag_list)
    step_size = 1.0 / jnp.sum(kernel * kernel, axis=(1, 2))
    weights = fit_bands(kernel, target, step_size)[:, :columns]
    return (structure, weights)


def solution(mesh):
    placed = (P(("tm", "qband"), None, None), P(), P(("tm", "qband"), None), P("tm", "qband"))
    return jax.shard_map(
        on_device,
        mesh=mesh,
        in_specs=placed,
        out_specs=(P(None, ("tm", "qband"), None), P("tm", "qband")),
        check_vma=False,
    )
```

```python
import math

import jax
import jax.numpy as jnp
from jax import lax
from jax.sharding import PartitionSpec as P
from jax.experimental import pallas as pl
from jax.experimental.pallas import tpu as pltpu

BINS = 1024
ITERS = 64
CHUNKS = 1
UNROLL = 8


def dft_table(length):
    positions = jnp.arange(length, dtype=jnp.int32)
    phase_index = positions[:, None] * positions[None, :] % length
    folded = jnp.minimum(phase_index, length - phase_index)
    sign_factor = jnp.where(phase_index * 2 > length, -1.0, 1.0).astype(jnp.float32)
    angles = folded.astype(jnp.float32) * (2.0 * math.pi / length)
    factor = 1.0 / math.sqrt(length)
    return jnp.concatenate(
        [jnp.cos(angles) * factor, -sign_factor * jnp.sin(angles) * factor], axis=1
    ).astype(jnp.bfloat16)


def structure_kernel(lags_ref, x_ref, out_ref, x32_ref):
    frames_all = x_ref.shape[0]
    pixels = out_ref.shape[2]

    def convert(t, carry):
        x32_ref[t] = x_ref[t].astype(jnp.float32)
        return carry

    lax.fori_loop(0, frames_all, convert, 0)

    def one_lag(l, carry):
        lag = lags_ref[l]
        count = frames_all - lag

        def step(t, acc):
            d = x32_ref[t + lag] - x32_ref[t]
            return acc + d * d

        def step_block(i, acc):
            for u in range(UNROLL):
                acc = step(i * UNROLL + u, acc)
            return acc

        blocks = count // UNROLL
        acc = lax.fori_loop(0, blocks, step_block, jnp.zeros(x32_ref.shape[1:], jnp.float32))
        acc = lax.fori_loop(blocks * UNROLL, count, step, acc)
        out_ref[l] = (acc[:, :pixels] + acc[:, pixels:]) / count.astype(jnp.float32)
        return carry

    lax.fori_loop(0, lags_ref.shape[0], one_lag, 0)


def structure_block(spectrum_block, lag_list):
    frames_all, rows, width = spectrum_block.shape
    nlag = lag_list.shape[0]
    return pl.pallas_call(
        structure_kernel,
        out_shape=jax.ShapeDtypeStruct((nlag, rows, width // 2), jnp.float32),
        in_specs=[
            pl.BlockSpec(memory_space=pltpu.SMEM),
            pl.BlockSpec(memory_space=pltpu.VMEM),
        ],
        out_specs=pl.BlockSpec(memory_space=pltpu.VMEM),
        scratch_shapes=[
            pltpu.VMEM((frames_all, rows, width), jnp.float32),
        ],
        compiler_params=pltpu.CompilerParams(vmem_limit_bytes=40 * 1024 * 1024),
    )(lag_list, spectrum_block)


def kernel_panel(decay_rates, lag_list):
    lag_values = lag_list.astype(jnp.float32)
    return (1.0 - jnp.exp(-decay_rates[:, None, :] * lag_values[None, :, None])) / BINS


def fit_kernel(k_ref, tgt_ref, step_ref, w_ref):
    panel = k_ref[...]
    tgt = tgt_ref[...][:, :, 0:1]
    step = step_ref[...]

    def body(i, w):
        predicted = jnp.sum(panel * w, axis=2, keepdims=True)
        residual = predicted - tgt
        gradient = jnp.sum(panel * residual, axis=1, keepdims=True)
        return jnp.maximum(w - step * gradient, 0.0)

    w_ref[...] = lax.fori_loop(0, ITERS, body, jnp.zeros(step.shape, jnp.float32), unroll=16)


def fit_bands(kernel, target, step_size):
    bands, lags, bins = kernel.shape
    tgt = jnp.broadcast_to(target[:, :, None], (bands, lags, 128))
    step = jnp.broadcast_to(step_size[:, None, None], (bands, 1, bins))
    out = pl.pallas_call(
        fit_kernel,
        out_shape=jax.ShapeDtypeStruct((bands, 1, bins), jnp.float32),
    )(kernel, tgt, step)
    return out[:, 0, :]


def on_device(frames, lag_list, band_index, decay_rates):
    pixels = frames.shape[1]
    devices = lax.axis_size(("tm", "qband"))
    table = lax.optimization_barrier(dft_table(pixels))
    row_transform = jnp.dot(frames[0], table, preferred_element_type=jnp.float32).astype(jnp.bfloat16)
    row_transform = row_transform.reshape(pixels, 2, pixels)
    cos_part = table[:, :pixels]
    sin_part = table[:, pixels:]
    width = pixels // CHUNKS
    pieces_out = []
    for k in range(CHUNKS):
        cols = slice(k * width, (k + 1) * width)
        mixing = jnp.stack([
            jnp.concatenate([cos_part[:, cols], sin_part[:, cols]], axis=1),
            jnp.concatenate([-sin_part[:, cols], cos_part[:, cols]], axis=1),
        ])
        spectrum = jnp.einsum("ypk,pyj->kj", row_transform, mixing, preferred_element_type=jnp.float32)
        spectrum = spectrum.astype(jnp.bfloat16).reshape(devices, pixels // devices, 2 * width)
        gathered = lax.all_to_all(spectrum, ("tm", "qband"), 0, 0, tiled=True)
        pieces_out.append(structure_block(gathered, lag_list))
    structure = jnp.concatenate(pieces_out, axis=2)

    bands_dev = decay_rates.shape[0]
    groups = lax.axis_size("tm")
    dest_band = (jnp.arange(devices, dtype=jnp.int32) // (devices // groups))[:, None] * bands_dev + jnp.arange(
        bands_dev, dtype=jnp.int32
    )[None, :]
    dest_hot = (band_index[:, 0][None, None, :] == dest_band[:, :, None]).astype(jnp.float32)
    dest_counts = jnp.sum(dest_hot, axis=2, keepdims=True)
    row_sums = jnp.sum(structure, axis=2)
    dest_totals = jnp.einsum("dbr,lr->dbl", dest_hot, row_sums, precision=lax.Precision.HIGHEST)
    per_dest = jnp.concatenate([dest_totals, dest_counts], axis=2)
    received = lax.all_to_all(per_dest, ("tm", "qband"), 0, 0, tiled=True)
    own = jnp.sum(received, axis=0)
    nlag = lag_list.shape[0]
    target = own[:, :nlag] / (own[:, nlag:] * pixels)

    columns = decay_rates.shape[1]
    ring = lax.axis_size("qband")
    pieces = [decay_rates] + [
        lax.ppermute(decay_rates, "qband", [(j, (j + s) % ring) for j in range(ring)]) for s in range(1, ring)
    ]
    all_rates = jnp.concatenate(pieces, axis=1)
    kernel = kernel_panel(all_rates, lag_list)
    step_size = 1.0 / jnp.sum(kernel * kernel, axis=(1, 2))
    weights = fit_bands(kernel, target, step_size)[:, :columns]
    return (structure, weights)


def solution(mesh):
    placed = (P(("tm", "qband"), None, None), P(), P(("tm", "qband"), None), P("tm", "qband"))
    return jax.shard_map(
        on_device,
        mesh=mesh,
        in_specs=placed,
        out_specs=(P(None, ("tm", "qband"), None), P("tm", "qband")),
        check_vma=False,
    )
```

```python
import math

import jax
import jax.numpy as jnp
from jax import lax
from jax.sharding import PartitionSpec as P
from jax.experimental import pallas as pl
from jax.experimental.pallas import tpu as pltpu

BINS = 1024
ITERS = 64
CHUNKS = 1
UNROLL = 8


def dft_table(length):
    positions = jnp.arange(length, dtype=jnp.int32)
    phase_index = positions[:, None] * positions[None, :] % length
    folded = jnp.minimum(phase_index, length - phase_index)
    sign_factor = jnp.where(phase_index * 2 > length, -1.0, 1.0).astype(jnp.float32)
    angles = folded.astype(jnp.float32) * (2.0 * math.pi / length)
    factor = 1.0 / math.sqrt(length)
    return jnp.concatenate(
        [jnp.cos(angles) * factor, -sign_factor * jnp.sin(angles) * factor], axis=1
    ).astype(jnp.bfloat16)


def structure_kernel(lags_ref, x_ref, out_ref, x32_ref):
    frames_all = x_ref.shape[0]
    pixels = out_ref.shape[2]

    def convert(t, carry):
        x32_ref[t] = x_ref[t].astype(jnp.float32)
        return carry

    lax.fori_loop(0, frames_all, convert, 0)

    def one_lag(l, carry):
        lag = lags_ref[l]
        count = frames_all - lag

        def step(t, acc):
            d = x32_ref[t + lag] - x32_ref[t]
            return acc + d * d

        def step_block(i, acc):
            for u in range(UNROLL):
                acc = step(i * UNROLL + u, acc)
            return acc

        blocks = count // UNROLL
        acc = lax.fori_loop(0, blocks, step_block, jnp.zeros(x32_ref.shape[1:], jnp.float32))
        acc = lax.fori_loop(blocks * UNROLL, count, step, acc)
        out_ref[l] = (acc[:, :pixels] + acc[:, pixels:]) / count.astype(jnp.float32)
        return carry

    lax.fori_loop(0, lags_ref.shape[0], one_lag, 0)


def structure_block(spectrum_block, lag_list):
    frames_all, rows, width = spectrum_block.shape
    nlag = lag_list.shape[0]
    return pl.pallas_call(
        structure_kernel,
        out_shape=jax.ShapeDtypeStruct((nlag, rows, width // 2), jnp.float32),
        in_specs=[
            pl.BlockSpec(memory_space=pltpu.SMEM),
            pl.BlockSpec(memory_space=pltpu.VMEM),
        ],
        out_specs=pl.BlockSpec(memory_space=pltpu.VMEM),
        scratch_shapes=[
            pltpu.VMEM((frames_all, rows, width), jnp.float32),
        ],
        compiler_params=pltpu.CompilerParams(vmem_limit_bytes=40 * 1024 * 1024),
    )(lag_list, spectrum_block)


def kernel_panel(decay_rates, lag_list):
    lag_values = lag_list.astype(jnp.float32)
    return (1.0 - jnp.exp(-decay_rates[:, None, :] * lag_values[None, :, None])) / BINS


def fit_kernel(k_ref, tgt_ref, w_ref):
    panel = k_ref[...]
    tgt = tgt_ref[...][:, :, 0:1]
    norm = jnp.sum(jnp.sum(panel * panel, axis=2, keepdims=True), axis=1, keepdims=True)
    step = 1.0 / norm

    def body(i, w):
        predicted = jnp.sum(panel * w, axis=2, keepdims=True)
        residual = predicted - tgt
        gradient = jnp.sum(panel * residual, axis=1, keepdims=True)
        return jnp.maximum(w - step * gradient, 0.0)

    shape = (panel.shape[0], 1, panel.shape[2])
    w = lax.fori_loop(0, ITERS, body, jnp.zeros(shape, jnp.float32), unroll=16)
    columns = w_ref.shape[1]
    for b in range(panel.shape[0]):
        w_ref[b:b + 1, :] = w[b, :, 0:columns]


def fit_bands(kernel, target, columns):
    bands, lags, bins = kernel.shape
    tgt = jnp.broadcast_to(target[:, :, None], (bands, lags, 128))
    return pl.pallas_call(
        fit_kernel,
        out_shape=jax.ShapeDtypeStruct((bands, columns), jnp.float32),
    )(kernel, tgt)


def on_device(frames, lag_list, band_index, decay_rates):
    pixels = frames.shape[1]
    devices = lax.axis_size(("tm", "qband"))
    table = lax.optimization_barrier(dft_table(pixels))
    row_transform = jnp.dot(frames[0], table, preferred_element_type=jnp.float32).astype(jnp.bfloat16)
    row_transform = row_transform.reshape(pixels, 2, pixels)
    cos_part = table[:, :pixels]
    sin_part = table[:, pixels:]
    width = pixels // CHUNKS
    pieces_out = []
    for k in range(CHUNKS):
        cols = slice(k * width, (k + 1) * width)
        mixing = jnp.stack([
            jnp.concatenate([cos_part[:, cols], sin_part[:, cols]], axis=1),
            jnp.concatenate([-sin_part[:, cols], cos_part[:, cols]], axis=1),
        ])
        spectrum = jnp.einsum("ypk,pyj->kj", row_transform, mixing, preferred_element_type=jnp.float32)
        spectrum = spectrum.astype(jnp.bfloat16).reshape(devices, pixels // devices, 2 * width)
        gathered = lax.all_to_all(spectrum, ("tm", "qband"), 0, 0, tiled=True)
        pieces_out.append(structure_block(gathered, lag_list))
    structure = jnp.concatenate(pieces_out, axis=2)

    bands_dev = decay_rates.shape[0]
    groups = lax.axis_size("tm")
    dest_band = (jnp.arange(devices, dtype=jnp.int32) // (devices // groups))[:, None] * bands_dev + jnp.arange(
        bands_dev, dtype=jnp.int32
    )[None, :]
    dest_hot = (band_index[:, 0][None, None, :] == dest_band[:, :, None]).astype(jnp.float32)
    dest_counts = jnp.sum(dest_hot, axis=2, keepdims=True)
    row_sums = jnp.sum(structure, axis=2)
    dest_totals = jnp.einsum("dbr,lr->dbl", dest_hot, row_sums, precision=lax.Precision.HIGHEST)
    per_dest = jnp.concatenate([dest_totals, dest_counts], axis=2)
    received = lax.all_to_all(per_dest, ("tm", "qband"), 0, 0, tiled=True)
    own = jnp.sum(received, axis=0)
    nlag = lag_list.shape[0]
    target = own[:, :nlag] / (own[:, nlag:] * pixels)

    columns = decay_rates.shape[1]
    ring = lax.axis_size("qband")
    pieces = [decay_rates] + [
        lax.ppermute(decay_rates, "qband", [(j, (j + s) % ring) for j in range(ring)]) for s in range(1, ring)
    ]
    all_rates = jnp.concatenate(pieces, axis=1)
    kernel = kernel_panel(all_rates, lag_list)
    weights = fit_bands(kernel, target, columns)
    return (structure, weights)


def solution(mesh):
    placed = (P(("tm", "qband"), None, None), P(), P(("tm", "qband"), None), P("tm", "qband"))
    return jax.shard_map(
        on_device,
        mesh=mesh,
        in_specs=placed,
        out_specs=(P(None, ("tm", "qband"), None), P("tm", "qband")),
        check_vma=False,
    )
```

```python
import math

import jax
import jax.numpy as jnp
from jax import lax
from jax.sharding import PartitionSpec as P
from jax.experimental import pallas as pl
from jax.experimental.pallas import tpu as pltpu

BINS = 1024
ITERS = 64
CHUNKS = 1
UNROLL = 8


def dft_table(length):
    positions = jnp.arange(length, dtype=jnp.int32)
    phase_index = positions[:, None] * positions[None, :] % length
    folded = jnp.minimum(phase_index, length - phase_index)
    sign_factor = jnp.where(phase_index * 2 > length, -1.0, 1.0).astype(jnp.float32)
    angles = folded.astype(jnp.float32) * (2.0 * math.pi / length)
    factor = 1.0 / math.sqrt(length)
    return jnp.concatenate(
        [jnp.cos(angles) * factor, -sign_factor * jnp.sin(angles) * factor], axis=1
    ).astype(jnp.bfloat16)


def structure_kernel(lags_ref, x_ref, out_ref, x32_ref):
    frames_all = x_ref.shape[0]
    pixels = out_ref.shape[2]

    def convert(t, carry):
        x32_ref[t] = x_ref[t].astype(jnp.float32)
        return carry

    lax.fori_loop(0, frames_all, convert, 0)

    def one_lag(l, carry):
        lag = lags_ref[l]
        count = frames_all - lag

        def step(t, acc):
            d = x32_ref[t + lag] - x32_ref[t]
            return acc + d * d

        def step_block(i, acc):
            for u in range(UNROLL):
                acc = step(i * UNROLL + u, acc)
            return acc

        blocks = count // UNROLL
        acc = lax.fori_loop(0, blocks, step_block, jnp.zeros(x32_ref.shape[1:], jnp.float32))
        acc = lax.fori_loop(blocks * UNROLL, count, step, acc)
        out_ref[l] = (acc[:, :pixels] + acc[:, pixels:]) / count.astype(jnp.float32)
        return carry

    lax.fori_loop(0, lags_ref.shape[0], one_lag, 0)


def structure_block(spectrum_block, lag_list):
    frames_all, rows, width = spectrum_block.shape
    nlag = lag_list.shape[0]
    return pl.pallas_call(
        structure_kernel,
        out_shape=jax.ShapeDtypeStruct((nlag, rows, width // 2), jnp.float32),
        in_specs=[
            pl.BlockSpec(memory_space=pltpu.SMEM),
            pl.BlockSpec(memory_space=pltpu.VMEM),
        ],
        out_specs=pl.BlockSpec(memory_space=pltpu.VMEM),
        scratch_shapes=[
            pltpu.VMEM((frames_all, rows, width), jnp.float32),
        ],
        compiler_params=pltpu.CompilerParams(vmem_limit_bytes=40 * 1024 * 1024),
    )(lag_list, spectrum_block)


def kernel_panel(decay_rates, lag_list):
    lag_values = lag_list.astype(jnp.float32)
    return (1.0 - jnp.exp(-decay_rates[:, None, :] * lag_values[None, :, None])) / BINS


def fit_kernel(k_ref, tgt_ref, w_ref):
    panel = k_ref[...]
    tgt = tgt_ref[...][:, :, 0:1]
    norm = jnp.sum(jnp.sum(panel * panel, axis=2, keepdims=True), axis=1, keepdims=True)
    step = 1.0 / norm

    def body(i, w):
        predicted = jnp.sum(panel * w, axis=2, keepdims=True)
        residual = predicted - tgt
        gradient = jnp.sum(panel * residual, axis=1, keepdims=True)
        return jnp.maximum(w - step * gradient, 0.0)

    shape = (panel.shape[0], 1, panel.shape[2])
    w = lax.fori_loop(0, ITERS, body, jnp.zeros(shape, jnp.float32), unroll=64)
    columns = w_ref.shape[1]
    for b in range(panel.shape[0]):
        w_ref[b:b + 1, :] = w[b, :, 0:columns]


def fit_bands(kernel, target, columns):
    bands, lags, bins = kernel.shape
    tgt = jnp.broadcast_to(target[:, :, None], (bands, lags, 128))
    return pl.pallas_call(
        fit_kernel,
        out_shape=jax.ShapeDtypeStruct((bands, columns), jnp.float32),
    )(kernel, tgt)


def on_device(frames, lag_list, band_index, decay_rates):
    pixels = frames.shape[1]
    devices = lax.axis_size(("tm", "qband"))
    table = lax.optimization_barrier(dft_table(pixels))
    row_transform = jnp.dot(frames[0], table, preferred_element_type=jnp.float32).astype(jnp.bfloat16)
    row_transform = row_transform.reshape(pixels, 2, pixels)
    cos_part = table[:, :pixels]
    sin_part = table[:, pixels:]
    width = pixels // CHUNKS
    pieces_out = []
    for k in range(CHUNKS):
        cols = slice(k * width, (k + 1) * width)
        mixing = jnp.stack([
            jnp.concatenate([cos_part[:, cols], sin_part[:, cols]], axis=1),
            jnp.concatenate([-sin_part[:, cols], cos_part[:, cols]], axis=1),
        ])
        spectrum = jnp.einsum("ypk,pyj->kj", row_transform, mixing, preferred_element_type=jnp.float32)
        spectrum = spectrum.astype(jnp.bfloat16).reshape(devices, pixels // devices, 2 * width)
        gathered = lax.all_to_all(spectrum, ("tm", "qband"), 0, 0, tiled=True)
        pieces_out.append(structure_block(gathered, lag_list))
    structure = jnp.concatenate(pieces_out, axis=2)

    bands_dev = decay_rates.shape[0]
    groups = lax.axis_size("tm")
    dest_band = (jnp.arange(devices, dtype=jnp.int32) // (devices // groups))[:, None] * bands_dev + jnp.arange(
        bands_dev, dtype=jnp.int32
    )[None, :]
    dest_hot = (band_index[:, 0][None, None, :] == dest_band[:, :, None]).astype(jnp.float32)
    dest_counts = jnp.sum(dest_hot, axis=2, keepdims=True)
    row_sums = jnp.sum(structure, axis=2)
    dest_totals = jnp.einsum("dbr,lr->dbl", dest_hot, row_sums, precision=lax.Precision.HIGHEST)
    per_dest = jnp.concatenate([dest_totals, dest_counts], axis=2)
    received = lax.all_to_all(per_dest, ("tm", "qband"), 0, 0, tiled=True)
    own = jnp.sum(received, axis=0)
    nlag = lag_list.shape[0]
    target = own[:, :nlag] / (own[:, nlag:] * pixels)

    columns = decay_rates.shape[1]
    ring = lax.axis_size("qband")
    pieces = [decay_rates] + [
        lax.ppermute(decay_rates, "qband", [(j, (j + s) % ring) for j in range(ring)]) for s in range(1, ring)
    ]
    all_rates = jnp.concatenate(pieces, axis=1)
    kernel = kernel_panel(all_rates, lag_list)
    weights = fit_bands(kernel, target, columns)
    return (structure, weights)


def solution(mesh):
    placed = (P(("tm", "qband"), None, None), P(), P(("tm", "qband"), None), P("tm", "qband"))
    return jax.shard_map(
        on_device,
        mesh=mesh,
        in_specs=placed,
        out_specs=(P(None, ("tm", "qband"), None), P("tm", "qband")),
        check_vma=False,
    )
```

```python
import math

import jax
import jax.numpy as jnp
from jax import lax
from jax.sharding import PartitionSpec as P
from jax.experimental import pallas as pl
from jax.experimental.pallas import tpu as pltpu

BINS = 1024
ITERS = 64
CHUNKS = 1
UNROLL = 8


def dft_table(length):
    positions = jnp.arange(length, dtype=jnp.int32)
    phase_index = positions[:, None] * positions[None, :] % length
    folded = jnp.minimum(phase_index, length - phase_index)
    sign_factor = jnp.where(phase_index * 2 > length, -1.0, 1.0).astype(jnp.float32)
    angles = folded.astype(jnp.float32) * (2.0 * math.pi / length)
    factor = 1.0 / math.sqrt(length)
    return jnp.concatenate(
        [jnp.cos(angles) * factor, -sign_factor * jnp.sin(angles) * factor], axis=1
    ).astype(jnp.bfloat16)


def structure_kernel(lags_ref, x_ref, out_ref, x32_ref):
    frames_all = x_ref.shape[0]
    pixels = out_ref.shape[2]

    def convert(t, carry):
        x32_ref[t] = x_ref[t].astype(jnp.float32)
        return carry

    lax.fori_loop(0, frames_all, convert, 0)

    def one_pair(p, carry):
        lag_a = lags_ref[2 * p]
        lag_b = lags_ref[2 * p + 1]
        count_a = frames_all - lag_a
        count_b = frames_all - lag_b
        common = jnp.minimum(count_a, count_b)

        def step_pair(t, accs):
            acc_a, acc_b = accs
            base = x32_ref[t]
            d_a = x32_ref[t + lag_a] - base
            d_b = x32_ref[t + lag_b] - base
            return acc_a + d_a * d_a, acc_b + d_b * d_b

        def block_pair(i, accs):
            for u in range(UNROLL):
                accs = step_pair(i * UNROLL + u, accs)
            return accs

        def step_one(lag):
            def step(t, acc):
                d = x32_ref[t + lag] - x32_ref[t]
                return acc + d * d
            return step

        zeros = jnp.zeros(x32_ref.shape[1:], jnp.float32)
        blocks = common // UNROLL
        acc_a, acc_b = lax.fori_loop(0, blocks, block_pair, (zeros, zeros))
        acc_a, acc_b = lax.fori_loop(blocks * UNROLL, common, step_pair, (acc_a, acc_b))
        acc_a = lax.fori_loop(common, count_a, step_one(lag_a), acc_a)
        acc_b = lax.fori_loop(common, count_b, step_one(lag_b), acc_b)
        out_ref[2 * p] = (acc_a[:, :pixels] + acc_a[:, pixels:]) / count_a.astype(jnp.float32)
        out_ref[2 * p + 1] = (acc_b[:, :pixels] + acc_b[:, pixels:]) / count_b.astype(jnp.float32)
        return carry

    lax.fori_loop(0, lags_ref.shape[0] // 2, one_pair, 0)


def structure_block(spectrum_block, lag_list):
    frames_all, rows, width = spectrum_block.shape
    nlag = lag_list.shape[0]
    return pl.pallas_call(
        structure_kernel,
        out_shape=jax.ShapeDtypeStruct((nlag, rows, width // 2), jnp.float32),
        in_specs=[
            pl.BlockSpec(memory_space=pltpu.SMEM),
            pl.BlockSpec(memory_space=pltpu.VMEM),
        ],
        out_specs=pl.BlockSpec(memory_space=pltpu.VMEM),
        scratch_shapes=[
            pltpu.VMEM((frames_all, rows, width), jnp.float32),
        ],
        compiler_params=pltpu.CompilerParams(vmem_limit_bytes=40 * 1024 * 1024),
    )(lag_list, spectrum_block)


def kernel_panel(decay_rates, lag_list):
    lag_values = lag_list.astype(jnp.float32)
    return (1.0 - jnp.exp(-decay_rates[:, None, :] * lag_values[None, :, None])) / BINS


def fit_kernel(k_ref, tgt_ref, w_ref):
    panel = k_ref[...]
    tgt = tgt_ref[...][:, :, 0:1]
    norm = jnp.sum(jnp.sum(panel * panel, axis=2, keepdims=True), axis=1, keepdims=True)
    step = 1.0 / norm

    def body(i, w):
        predicted = jnp.sum(panel * w, axis=2, keepdims=True)
        residual = predicted - tgt
        gradient = jnp.sum(panel * residual, axis=1, keepdims=True)
        return jnp.maximum(w - step * gradient, 0.0)

    shape = (panel.shape[0], 1, panel.shape[2])
    w = lax.fori_loop(0, ITERS, body, jnp.zeros(shape, jnp.float32), unroll=16)
    columns = w_ref.shape[1]
    for b in range(panel.shape[0]):
        w_ref[b:b + 1, :] = w[b, :, 0:columns]


def fit_bands(kernel, target, columns):
    bands, lags, bins = kernel.shape
    tgt = jnp.broadcast_to(target[:, :, None], (bands, lags, 128))
    return pl.pallas_call(
        fit_kernel,
        out_shape=jax.ShapeDtypeStruct((bands, columns), jnp.float32),
    )(kernel, tgt)


def on_device(frames, lag_list, band_index, decay_rates):
    pixels = frames.shape[1]
    devices = lax.axis_size(("tm", "qband"))
    table = lax.optimization_barrier(dft_table(pixels))
    row_transform = jnp.dot(frames[0], table, preferred_element_type=jnp.float32).astype(jnp.bfloat16)
    row_transform = row_transform.reshape(pixels, 2, pixels)
    cos_part = table[:, :pixels]
    sin_part = table[:, pixels:]
    width = pixels // CHUNKS
    pieces_out = []
    for k in range(CHUNKS):
        cols = slice(k * width, (k + 1) * width)
        mixing = jnp.stack([
            jnp.concatenate([cos_part[:, cols], sin_part[:, cols]], axis=1),
            jnp.concatenate([-sin_part[:, cols], cos_part[:, cols]], axis=1),
        ])
        spectrum = jnp.einsum("ypk,pyj->kj", row_transform, mixing, preferred_element_type=jnp.float32)
        spectrum = spectrum.astype(jnp.bfloat16).reshape(devices, pixels // devices, 2 * width)
        gathered = lax.all_to_all(spectrum, ("tm", "qband"), 0, 0, tiled=True)
        pieces_out.append(structure_block(gathered, lag_list))
    structure = jnp.concatenate(pieces_out, axis=2)

    bands_dev = decay_rates.shape[0]
    groups = lax.axis_size("tm")
    dest_band = (jnp.arange(devices, dtype=jnp.int32) // (devices // groups))[:, None] * bands_dev + jnp.arange(
        bands_dev, dtype=jnp.int32
    )[None, :]
    dest_hot = (band_index[:, 0][None, None, :] == dest_band[:, :, None]).astype(jnp.float32)
    dest_counts = jnp.sum(dest_hot, axis=2, keepdims=True)
    row_sums = jnp.sum(structure, axis=2)
    dest_totals = jnp.einsum("dbr,lr->dbl", dest_hot, row_sums, precision=lax.Precision.HIGHEST)
    per_dest = jnp.concatenate([dest_totals, dest_counts], axis=2)
    received = lax.all_to_all(per_dest, ("tm", "qband"), 0, 0, tiled=True)
    own = jnp.sum(received, axis=0)
    nlag = lag_list.shape[0]
    target = own[:, :nlag] / (own[:, nlag:] * pixels)

    columns = decay_rates.shape[1]
    ring = lax.axis_size("qband")
    pieces = [decay_rates] + [
        lax.ppermute(decay_rates, "qband", [(j, (j + s) % ring) for j in range(ring)]) for s in range(1, ring)
    ]
    all_rates = jnp.concatenate(pieces, axis=1)
    kernel = kernel_panel(all_rates, lag_list)
    weights = fit_bands(kernel, target, columns)
    return (structure, weights)


def solution(mesh):
    placed = (P(("tm", "qband"), None, None), P(), P(("tm", "qband"), None), P("tm", "qband"))
    return jax.shard_map(
        on_device,
        mesh=mesh,
        in_specs=placed,
        out_specs=(P(None, ("tm", "qband"), None), P("tm", "qband")),
        check_vma=False,
    )
```

```python
import math

import jax
import jax.numpy as jnp
from jax import lax
from jax.sharding import PartitionSpec as P
from jax.experimental import pallas as pl
from jax.experimental.pallas import tpu as pltpu

BINS = 1024
ITERS = 64
CHUNKS = 1
UNROLL = 8


def dft_table(length):
    positions = jnp.arange(length, dtype=jnp.int32)
    phase_index = positions[:, None] * positions[None, :] % length
    folded = jnp.minimum(phase_index, length - phase_index)
    sign_factor = jnp.where(phase_index * 2 > length, -1.0, 1.0).astype(jnp.float32)
    angles = folded.astype(jnp.float32) * (2.0 * math.pi / length)
    factor = 1.0 / math.sqrt(length)
    return jnp.concatenate(
        [jnp.cos(angles) * factor, -sign_factor * jnp.sin(angles) * factor], axis=1
    ).astype(jnp.bfloat16)


def structure_kernel(lags_ref, x_ref, out_ref, rows_ref, x32_ref):
    frames_all = x_ref.shape[0]
    pixels = out_ref.shape[2]

    def convert(t, carry):
        x32_ref[t] = x_ref[t].astype(jnp.float32)
        return carry

    lax.fori_loop(0, frames_all, convert, 0)

    def one_lag(l, carry):
        lag = lags_ref[l]
        count = frames_all - lag

        def step(t, acc):
            d = x32_ref[t + lag] - x32_ref[t]
            return acc + d * d

        def step_block(i, acc):
            for u in range(UNROLL):
                acc = step(i * UNROLL + u, acc)
            return acc

        blocks = count // UNROLL
        acc = lax.fori_loop(0, blocks, step_block, jnp.zeros(x32_ref.shape[1:], jnp.float32))
        acc = lax.fori_loop(blocks * UNROLL, count, step, acc)
        value = (acc[:, :pixels] + acc[:, pixels:]) / count.astype(jnp.float32)
        out_ref[l] = value
        part = value[:, 0:128]
        for i in range(1, pixels // 128):
            part = part + value[:, i * 128:(i + 1) * 128]
        rows_ref[l] = part
        return carry

    lax.fori_loop(0, lags_ref.shape[0], one_lag, 0)


def structure_block(spectrum_block, lag_list):
    frames_all, rows, width = spectrum_block.shape
    nlag = lag_list.shape[0]
    return pl.pallas_call(
        structure_kernel,
        out_shape=(
            jax.ShapeDtypeStruct((nlag, rows, width // 2), jnp.float32),
            jax.ShapeDtypeStruct((nlag, rows, 128), jnp.float32),
        ),
        in_specs=[
            pl.BlockSpec(memory_space=pltpu.SMEM),
            pl.BlockSpec(memory_space=pltpu.VMEM),
        ],
        out_specs=(pl.BlockSpec(memory_space=pltpu.VMEM), pl.BlockSpec(memory_space=pltpu.VMEM)),
        scratch_shapes=[
            pltpu.VMEM((frames_all, rows, width), jnp.float32),
        ],
        compiler_params=pltpu.CompilerParams(vmem_limit_bytes=40 * 1024 * 1024),
    )(lag_list, spectrum_block)


def kernel_panel(decay_rates, lag_list):
    lag_values = lag_list.astype(jnp.float32)
    return (1.0 - jnp.exp(-decay_rates[:, None, :] * lag_values[None, :, None])) / BINS


def fit_kernel(k_ref, tgt_ref, w_ref):
    panel = k_ref[...]
    tgt = tgt_ref[...][:, :, 0:1]
    norm = jnp.sum(jnp.sum(panel * panel, axis=2, keepdims=True), axis=1, keepdims=True)
    step = 1.0 / norm

    def body(i, w):
        predicted = jnp.sum(panel * w, axis=2, keepdims=True)
        residual = predicted - tgt
        gradient = jnp.sum(panel * residual, axis=1, keepdims=True)
        return jnp.maximum(w - step * gradient, 0.0)

    shape = (panel.shape[0], 1, panel.shape[2])
    w = lax.fori_loop(0, ITERS, body, jnp.zeros(shape, jnp.float32), unroll=16)
    columns = w_ref.shape[1]
    for b in range(panel.shape[0]):
        w_ref[b:b + 1, :] = w[b, :, 0:columns]


def fit_bands(kernel, target, columns):
    bands, lags, bins = kernel.shape
    tgt = jnp.broadcast_to(target[:, :, None], (bands, lags, 128))
    return pl.pallas_call(
        fit_kernel,
        out_shape=jax.ShapeDtypeStruct((bands, columns), jnp.float32),
    )(kernel, tgt)


def on_device(frames, lag_list, band_index, decay_rates):
    pixels = frames.shape[1]
    devices = lax.axis_size(("tm", "qband"))
    table = lax.optimization_barrier(dft_table(pixels))
    row_transform = jnp.dot(frames[0], table, preferred_element_type=jnp.float32).astype(jnp.bfloat16)
    row_transform = row_transform.reshape(pixels, 2, pixels)
    cos_part = table[:, :pixels]
    sin_part = table[:, pixels:]
    width = pixels // CHUNKS
    pieces_out = []
    partials = []
    for k in range(CHUNKS):
        cols = slice(k * width, (k + 1) * width)
        mixing = jnp.stack([
            jnp.concatenate([cos_part[:, cols], sin_part[:, cols]], axis=1),
            jnp.concatenate([-sin_part[:, cols], cos_part[:, cols]], axis=1),
        ])
        spectrum = jnp.einsum("ypk,pyj->kj", row_transform, mixing, preferred_element_type=jnp.float32)
        spectrum = spectrum.astype(jnp.bfloat16).reshape(devices, pixels // devices, 2 * width)
        gathered = lax.all_to_all(spectrum, ("tm", "qband"), 0, 0, tiled=True)
        piece, partial = structure_block(gathered, lag_list)
        pieces_out.append(piece)
        partials.append(partial)
    structure = jnp.concatenate(pieces_out, axis=2)

    bands_dev = decay_rates.shape[0]
    groups = lax.axis_size("tm")
    dest_band = (jnp.arange(devices, dtype=jnp.int32) // (devices // groups))[:, None] * bands_dev + jnp.arange(
        bands_dev, dtype=jnp.int32
    )[None, :]
    dest_hot = (band_index[:, 0][None, None, :] == dest_band[:, :, None]).astype(jnp.float32)
    dest_counts = jnp.sum(dest_hot, axis=2, keepdims=True)
    row_sums = jnp.sum(jnp.concatenate(partials, axis=2), axis=2)
    dest_totals = jnp.einsum("dbr,lr->dbl", dest_hot, row_sums, precision=lax.Precision.HIGHEST)
    per_dest = jnp.concatenate([dest_totals, dest_counts], axis=2)
    received = lax.all_to_all(per_dest, ("tm", "qband"), 0, 0, tiled=True)
    own = jnp.sum(received, axis=0)
    nlag = lag_list.shape[0]
    target = own[:, :nlag] / (own[:, nlag:] * pixels)

    columns = decay_rates.shape[1]
    ring = lax.axis_size("qband")
    pieces = [decay_rates] + [
        lax.ppermute(decay_rates, "qband", [(j, (j + s) % ring) for j in range(ring)]) for s in range(1, ring)
    ]
    all_rates = jnp.concatenate(pieces, axis=1)
    kernel = kernel_panel(all_rates, lag_list)
    weights = fit_bands(kernel, target, columns)
    return (structure, weights)


def solution(mesh):
    placed = (P(("tm", "qband"), None, None), P(), P(("tm", "qband"), None), P("tm", "qband"))
    return jax.shard_map(
        on_device,
        mesh=mesh,
        in_specs=placed,
        out_specs=(P(None, ("tm", "qband"), None), P("tm", "qband")),
        check_vma=False,
    )
```

```python
import math

import jax
import jax.numpy as jnp
from jax import lax
from jax.sharding import PartitionSpec as P
from jax.experimental import pallas as pl
from jax.experimental.pallas import tpu as pltpu

BINS = 1024
ITERS = 64
CHUNKS = 1
UNROLL = 8


def dft_table(length):
    positions = jnp.arange(length, dtype=jnp.int32)
    phase_index = positions[:, None] * positions[None, :] % length
    folded = jnp.minimum(phase_index, length - phase_index)
    sign_factor = jnp.where(phase_index * 2 > length, -1.0, 1.0).astype(jnp.float32)
    angles = folded.astype(jnp.float32) * (2.0 * math.pi / length)
    factor = 1.0 / math.sqrt(length)
    return jnp.concatenate(
        [jnp.cos(angles) * factor, -sign_factor * jnp.sin(angles) * factor], axis=1
    ).astype(jnp.bfloat16)


def structure_kernel(lags_ref, x_ref, out_ref, rows_ref, x32_ref):
    frames_all = x_ref.shape[0]
    pixels = out_ref.shape[2]

    def convert(t, carry):
        x32_ref[t] = x_ref[t].astype(jnp.float32)
        return carry

    lax.fori_loop(0, frames_all, convert, 0)

    def one_lag(l, carry):
        lag = lags_ref[l]
        count = frames_all - lag

        def step(t, acc):
            d = x32_ref[t + lag] - x32_ref[t]
            return acc + d * d

        def step_block(i, acc):
            for u in range(UNROLL):
                acc = step(i * UNROLL + u, acc)
            return acc

        blocks = count // UNROLL
        acc = lax.fori_loop(0, blocks, step_block, jnp.zeros(x32_ref.shape[1:], jnp.float32))
        acc = lax.fori_loop(blocks * UNROLL, count, step, acc)
        value = (acc[:, :pixels] + acc[:, pixels:]) / count.astype(jnp.float32)
        out_ref[l] = value
        part = value[:, 0:128]
        for i in range(1, pixels // 128):
            part = part + value[:, i * 128:(i + 1) * 128]
        rows_ref[l] = part
        return carry

    lax.fori_loop(0, lags_ref.shape[0], one_lag, 0)


def structure_block(spectrum_block, lag_list):
    frames_all, rows, width = spectrum_block.shape
    nlag = lag_list.shape[0]
    return pl.pallas_call(
        structure_kernel,
        out_shape=(
            jax.ShapeDtypeStruct((nlag, rows, width // 2), jnp.float32),
            jax.ShapeDtypeStruct((nlag, rows, 128), jnp.float32),
        ),
        in_specs=[
            pl.BlockSpec(memory_space=pltpu.SMEM),
            pl.BlockSpec(memory_space=pltpu.VMEM),
        ],
        out_specs=(pl.BlockSpec(memory_space=pltpu.VMEM), pl.BlockSpec(memory_space=pltpu.VMEM)),
        scratch_shapes=[
            pltpu.VMEM((frames_all, rows, width), jnp.float32),
        ],
        compiler_params=pltpu.CompilerParams(vmem_limit_bytes=40 * 1024 * 1024),
    )(lag_list, spectrum_block)


def kernel_panel(decay_rates, lag_list):
    lag_values = lag_list.astype(jnp.float32)
    return (1.0 - jnp.exp(-decay_rates[:, None, :] * lag_values[None, :, None])) / BINS


def fit_kernel(k_ref, tgt_ref, w_ref):
    panel = k_ref[...]
    tgt = tgt_ref[...][:, :, 0:1]
    norm = jnp.sum(jnp.sum(panel * panel, axis=2, keepdims=True), axis=1, keepdims=True)
    step = 1.0 / norm

    def body(i, w):
        predicted = jnp.sum(panel * w, axis=2, keepdims=True)
        residual = predicted - tgt
        gradient = jnp.sum(panel * residual, axis=1, keepdims=True)
        return jnp.maximum(w - step * gradient, 0.0)

    shape = (panel.shape[0], 1, panel.shape[2])
    w = lax.fori_loop(0, ITERS, body, jnp.zeros(shape, jnp.float32), unroll=16)
    columns = w_ref.shape[1]
    for b in range(panel.shape[0]):
        w_ref[b:b + 1, :] = w[b, :, 0:columns]


def fit_bands(kernel, target, columns):
    bands, lags, bins = kernel.shape
    tgt = target[:, :, None]
    return pl.pallas_call(
        fit_kernel,
        out_shape=jax.ShapeDtypeStruct((bands, columns), jnp.float32),
    )(kernel, tgt)


def on_device(frames, lag_list, band_index, decay_rates):
    pixels = frames.shape[1]
    devices = lax.axis_size(("tm", "qband"))
    table = lax.optimization_barrier(dft_table(pixels))
    row_transform = jnp.dot(frames[0], table, preferred_element_type=jnp.float32).astype(jnp.bfloat16)
    row_transform = row_transform.reshape(pixels, 2, pixels)
    cos_part = table[:, :pixels]
    sin_part = table[:, pixels:]
    width = pixels // CHUNKS
    pieces_out = []
    partials = []
    for k in range(CHUNKS):
        cols = slice(k * width, (k + 1) * width)
        mixing = jnp.stack([
            jnp.concatenate([cos_part[:, cols], sin_part[:, cols]], axis=1),
            jnp.concatenate([-sin_part[:, cols], cos_part[:, cols]], axis=1),
        ])
        spectrum = jnp.einsum("ypk,pyj->kj", row_transform, mixing, preferred_element_type=jnp.float32)
        spectrum = spectrum.astype(jnp.bfloat16).reshape(devices, pixels // devices, 2 * width)
        gathered = lax.all_to_all(spectrum, ("tm", "qband"), 0, 0, tiled=True)
        piece, partial = structure_block(gathered, lag_list)
        pieces_out.append(piece)
        partials.append(partial)
    structure = jnp.concatenate(pieces_out, axis=2)

    bands_dev = decay_rates.shape[0]
    groups = lax.axis_size("tm")
    dest_band = (jnp.arange(devices, dtype=jnp.int32) // (devices // groups))[:, None] * bands_dev + jnp.arange(
        bands_dev, dtype=jnp.int32
    )[None, :]
    dest_hot = (band_index[:, 0][None, None, :] == dest_band[:, :, None]).astype(jnp.float32)
    dest_counts = jnp.sum(dest_hot, axis=2, keepdims=True)
    row_sums = jnp.sum(jnp.concatenate(partials, axis=2), axis=2)
    dest_totals = jnp.einsum("dbr,lr->dbl", dest_hot, row_sums, precision=lax.Precision.HIGHEST)
    per_dest = jnp.concatenate([dest_totals, dest_counts], axis=2)
    received = lax.all_to_all(per_dest, ("tm", "qband"), 0, 0, tiled=True)
    own = jnp.sum(received, axis=0)
    nlag = lag_list.shape[0]
    target = own[:, :nlag] / (own[:, nlag:] * pixels)

    columns = decay_rates.shape[1]
    ring = lax.axis_size("qband")
    pieces = [decay_rates] + [
        lax.ppermute(decay_rates, "qband", [(j, (j + s) % ring) for j in range(ring)]) for s in range(1, ring)
    ]
    all_rates = jnp.concatenate(pieces, axis=1)
    kernel = kernel_panel(all_rates, lag_list)
    weights = fit_bands(kernel, target, columns)
    return (structure, weights)


def solution(mesh):
    placed = (P(("tm", "qband"), None, None), P(), P(("tm", "qband"), None), P("tm", "qband"))
    return jax.shard_map(
        on_device,
        mesh=mesh,
        in_specs=placed,
        out_specs=(P(None, ("tm", "qband"), None), P("tm", "qband")),
        check_vma=False,
    )
```

```python
import math

import jax
import jax.numpy as jnp
from jax import lax
from jax.sharding import PartitionSpec as P
from jax.experimental import pallas as pl
from jax.experimental.pallas import tpu as pltpu

BINS = 1024
ITERS = 64
CHUNKS = 1
UNROLL = 8


def dft_table(length):
    positions = jnp.arange(length, dtype=jnp.int32)
    phase_index = positions[:, None] * positions[None, :] % length
    folded = jnp.minimum(phase_index, length - phase_index)
    sign_factor = jnp.where(phase_index * 2 > length, -1.0, 1.0).astype(jnp.float32)
    angles = folded.astype(jnp.float32) * (2.0 * math.pi / length)
    factor = 1.0 / math.sqrt(length)
    return jnp.concatenate(
        [jnp.cos(angles) * factor, -sign_factor * jnp.sin(angles) * factor], axis=1
    ).astype(jnp.bfloat16)


def structure_kernel(lags_ref, x_ref, out_ref, rows_ref, x32_ref):
    frames_all = x_ref.shape[0]
    pixels = out_ref.shape[2]

    def convert(t, carry):
        x32_ref[t] = x_ref[t].astype(jnp.float32)
        return carry

    lax.fori_loop(0, frames_all, convert, 0, unroll=8)

    def one_lag(l, carry):
        lag = lags_ref[l]
        count = frames_all - lag

        def step(t, acc):
            d = x32_ref[t + lag] - x32_ref[t]
            return acc + d * d

        def step_block(i, acc):
            for u in range(UNROLL):
                acc = step(i * UNROLL + u, acc)
            return acc

        blocks = count // UNROLL
        acc = lax.fori_loop(0, blocks, step_block, jnp.zeros(x32_ref.shape[1:], jnp.float32))
        acc = lax.fori_loop(blocks * UNROLL, count, step, acc)
        value = (acc[:, :pixels] + acc[:, pixels:]) / count.astype(jnp.float32)
        out_ref[l] = value
        part = value[:, 0:128]
        for i in range(1, pixels // 128):
            part = part + value[:, i * 128:(i + 1) * 128]
        rows_ref[l] = part
        return carry

    lax.fori_loop(0, lags_ref.shape[0], one_lag, 0)


def structure_block(spectrum_block, lag_list):
    frames_all, rows, width = spectrum_block.shape
    nlag = lag_list.shape[0]
    return pl.pallas_call(
        structure_kernel,
        out_shape=(
            jax.ShapeDtypeStruct((nlag, rows, width // 2), jnp.float32),
            jax.ShapeDtypeStruct((nlag, rows, 128), jnp.float32),
        ),
        in_specs=[
            pl.BlockSpec(memory_space=pltpu.SMEM),
            pl.BlockSpec(memory_space=pltpu.VMEM),
        ],
        out_specs=(pl.BlockSpec(memory_space=pltpu.VMEM), pl.BlockSpec(memory_space=pltpu.VMEM)),
        scratch_shapes=[
            pltpu.VMEM((frames_all, rows, width), jnp.float32),
        ],
        compiler_params=pltpu.CompilerParams(vmem_limit_bytes=40 * 1024 * 1024),
    )(lag_list, spectrum_block)


def kernel_panel(decay_rates, lag_list):
    lag_values = lag_list.astype(jnp.float32)
    return (1.0 - jnp.exp(-decay_rates[:, None, :] * lag_values[None, :, None])) / BINS


def fit_kernel(k_ref, tgt_ref, w_ref):
    panel = k_ref[...]
    tgt = tgt_ref[...][:, :, 0:1]
    norm = jnp.sum(jnp.sum(panel * panel, axis=2, keepdims=True), axis=1, keepdims=True)
    step = 1.0 / norm

    def body(i, w):
        predicted = jnp.sum(panel * w, axis=2, keepdims=True)
        residual = predicted - tgt
        gradient = jnp.sum(panel * residual, axis=1, keepdims=True)
        return jnp.maximum(w - step * gradient, 0.0)

    shape = (panel.shape[0], 1, panel.shape[2])
    w = lax.fori_loop(0, ITERS, body, jnp.zeros(shape, jnp.float32), unroll=16)
    columns = w_ref.shape[1]
    for b in range(panel.shape[0]):
        w_ref[b:b + 1, :] = w[b, :, 0:columns]


def fit_bands(kernel, target, columns):
    bands, lags, bins = kernel.shape
    tgt = target[:, :, None]
    return pl.pallas_call(
        fit_kernel,
        out_shape=jax.ShapeDtypeStruct((bands, columns), jnp.float32),
    )(kernel, tgt)


def on_device(frames, lag_list, band_index, decay_rates):
    pixels = frames.shape[1]
    devices = lax.axis_size(("tm", "qband"))
    table = lax.optimization_barrier(dft_table(pixels))
    row_transform = jnp.dot(frames[0], table, preferred_element_type=jnp.float32).astype(jnp.bfloat16)
    row_transform = row_transform.reshape(pixels, 2, pixels)
    cos_part = table[:, :pixels]
    sin_part = table[:, pixels:]
    width = pixels // CHUNKS
    pieces_out = []
    partials = []
    for k in range(CHUNKS):
        cols = slice(k * width, (k + 1) * width)
        mixing = jnp.stack([
            jnp.concatenate([cos_part[:, cols], sin_part[:, cols]], axis=1),
            jnp.concatenate([-sin_part[:, cols], cos_part[:, cols]], axis=1),
        ])
        spectrum = jnp.einsum("ypk,pyj->kj", row_transform, mixing, preferred_element_type=jnp.float32)
        spectrum = spectrum.astype(jnp.bfloat16).reshape(devices, pixels // devices, 2 * width)
        gathered = lax.all_to_all(spectrum, ("tm", "qband"), 0, 0, tiled=True)
        piece, partial = structure_block(gathered, lag_list)
        pieces_out.append(piece)
        partials.append(partial)
    structure = jnp.concatenate(pieces_out, axis=2)

    bands_dev = decay_rates.shape[0]
    groups = lax.axis_size("tm")
    dest_band = (jnp.arange(devices, dtype=jnp.int32) // (devices // groups))[:, None] * bands_dev + jnp.arange(
        bands_dev, dtype=jnp.int32
    )[None, :]
    dest_hot = (band_index[:, 0][None, None, :] == dest_band[:, :, None]).astype(jnp.float32)
    dest_counts = jnp.sum(dest_hot, axis=2, keepdims=True)
    row_sums = jnp.sum(jnp.concatenate(partials, axis=2), axis=2)
    dest_totals = jnp.einsum("dbr,lr->dbl", dest_hot, row_sums, precision=lax.Precision.HIGHEST)
    per_dest = jnp.concatenate([dest_totals, dest_counts], axis=2)
    received = lax.all_to_all(per_dest, ("tm", "qband"), 0, 0, tiled=True)
    own = jnp.sum(received, axis=0)
    nlag = lag_list.shape[0]
    target = own[:, :nlag] / (own[:, nlag:] * pixels)

    columns = decay_rates.shape[1]
    ring = lax.axis_size("qband")
    pieces = [decay_rates] + [
        lax.ppermute(decay_rates, "qband", [(j, (j + s) % ring) for j in range(ring)]) for s in range(1, ring)
    ]
    all_rates = jnp.concatenate(pieces, axis=1)
    kernel = kernel_panel(all_rates, lag_list)
    weights = fit_bands(kernel, target, columns)
    return (structure, weights)


def solution(mesh):
    placed = (P(("tm", "qband"), None, None), P(), P(("tm", "qband"), None), P("tm", "qband"))
    return jax.shard_map(
        on_device,
        mesh=mesh,
        in_specs=placed,
        out_specs=(P(None, ("tm", "qband"), None), P("tm", "qband")),
        check_vma=False,
    )
```
